128 devices in a mesh: rows: 32 (over x, z, core), cols: 4 (over y).
Axes of the slice: x: 4, y: 4, z: 4, core: 2. Of those that a mesh axis runs over, the one named last changes fastest.
Arguments:
- land_jac: float32 [16, 3, 262144], P(None, None, ('rows', 'cols')), may hold values from -6 to 6, as said below
- pose_jac: float32 [16, 6, 262144], P(None, None, ('rows', 'cols')), may hold values from -2 to 2
- segment: int32 [8, 262144], P(None, ('rows', 'cols')), may hold values from 0 to 4
- knot_frac: float32 [8, 262144], P(None, ('rows', 'cols')), may hold values from 0 to 1
- track_len: int32 [262144], P(('rows', 'cols')), may hold values from 2 to 8
- block_base: int32 [2048], P(('rows', 'cols')), may hold values from 0 to 504, as said below
- damping: float32 [3072], P('cols'), may hold values from 0.15 to 1.5
Outputs:
- factors: float32 [3072, 768], P('cols')
The draws below stay inside these ranges and needn't reach their ends.
Inputs may be any that keep to these rules, and one draw needn't show every extreme that they name: `land_jac`: observation j's rows 2j and 2j+1 are s [1, 0, a] and s [0, 1, b] with s positive; a is below -0.5 at observation 0 and above 0.5 at observation 1. A block's window of 8 knots lies inside one group: block_base mod 128 is at most 120.
All inputs are finite; a program needn't handle non-finite values.
Results may differ from the reference program's by a relative error of at most 0.0003.
Values sent between devices are 32-bit elements; how exact they have to be, the bound alone decides.
No kernel may reach another device: no remote copies, remote signals or barrier semaphores. Data moves between devices by JAX's collectives and lax.ppermute only.
A program may use at most 320 MiB of HBM per device.

```python
import math
import jax
import jax.numpy as jnp
from jax import lax

KNOTS = 512
KDOF = 6
WIN_KNOTS = 8
OBS = 8
LBLK = 128
BLK_DEV = 16
C = 3072
GROUP_KNOTS = 128
CG = 768
BLOCKS = 2048
LANDMARKS = 262144
N_COLS = 4


def landmark_values(key):
    key_scale, key_across, key_nudge, key_upward = jax.random.split(key, 4)
    grid_shape = (OBS, LANDMARKS)
    spread = jnp.exp(jax.random.uniform(key_scale, grid_shape, jnp.float32, math.log(0.5), math.log(2.0)))
    wander = jax.random.uniform(key_across, grid_shape, jnp.float32, -1.5, 1.5)
    nudged = jax.random.uniform(key_nudge, grid_shape, jnp.float32, 0.0, 0.4)
    obs_rank = lax.broadcasted_iota(jnp.int32, grid_shape, 0)
    across = jnp.where(obs_rank == 0, -0.6 - nudged, jnp.where(obs_rank == 1, 0.6 + nudged, wander))
    upward = jax.random.uniform(key_upward, grid_shape, jnp.float32, -1.5, 1.5)
    nothing = jnp.zeros(grid_shape, jnp.float32)
    first_row = jnp.stack([spread, nothing, spread * across], axis=1)
    second_row = jnp.stack([nothing, spread, spread * upward], axis=1)
    return jnp.stack([first_row, second_row], axis=1).reshape(2 * OBS, 3, LANDMARKS)


def draw_land_jac(key, part):
    return landmark_values(key)


def draw_pose_jac(key, part):
    landmark = landmark_values(key)
    key_noise = jax.random.fold_in(key, 7)
    noise_scale = math.sqrt(160.0 / LANDMARKS)
    full_shape = (2 * OBS, KDOF, LANDMARKS)
    noise = jnp.clip(jax.random.normal(key_noise, full_shape, jnp.float32), -4.0, 4.0)
    noise = noise_scale * noise
    moving = -0.25 * landmark + 0.1 * noise[:, :3, :]
    return jnp.concatenate([moving, noise[:, 3:, :]], axis=1)


def draw_block_base(key, part):
    key_one, key_two, key_off = jax.random.split(key, 3)
    groups = KNOTS // GROUP_KNOTS
    draw_one = jax.random.randint(key_one, (BLOCKS,), 0, groups)
    draw_two = jax.random.randint(key_two, (BLOCKS,), 0, groups)
    group_id = jnp.minimum(draw_one, draw_two)
    offset = jax.random.randint(key_off, (BLOCKS,), 0, GROUP_KNOTS - WIN_KNOTS + 1)
    position = lax.broadcasted_iota(jnp.int32, (BLOCKS,), 0)
    group_id = jnp.where(position == 0, groups - 1, jnp.where(position == 1, 0, group_id))
    offset = jnp.where(position == 0, GROUP_KNOTS - WIN_KNOTS, jnp.where(position == 1, 0, offset))
    return (group_id * GROUP_KNOTS + offset).astype(jnp.int32)


def touch_ends(drawn, key, smallest, high):
    longest = drawn.shape.index(max(drawn.shape))
    spots = []
    for shift in (0, 1):
        where = [jax.random.randint(jax.random.fold_in(key, axis), (), 0, length) for axis, length in enumerate(drawn.shape)]
        where[longest] = (where[longest] + shift) % drawn.shape[longest]
        spots.append(tuple(where))
    return drawn.at[spots[0]].set(smallest).at[spots[1]].set(high)


def level_of(stream_key, dims, cuts, least, largest):
    def one(dim, parts):
        steps = jax.random.uniform(jax.random.fold_in(jax.random.fold_in(stream_key, 6), dim), (parts,), jnp.float32, least / len(cuts), largest / len(cuts))
        return jnp.repeat(jnp.exp(steps), dims[dim] // parts).reshape((-1,) + (1,) * (len(dims) - dim - 1))

    gain = one(*cuts[0])
    for cut in cuts[1:]:
        gain = gain * one(*cut)
    return gain


def setup_inputs(seed: int = 0) -> dict:
    splits = jax.random.split(jax.random.key(seed), 8)
    return {
        "land_jac": draw_land_jac(jax.random.fold_in(splits[7], 71), 0),
        "pose_jac": draw_pose_jac(jax.random.fold_in(splits[7], 71), 0),
        "segment": touch_ends(jax.random.randint(splits[2], (OBS, LANDMARKS), 0, WIN_KNOTS - 3), jax.random.fold_in(splits[2], 1), 0, (WIN_KNOTS - 3) - 1).astype(jnp.int32),
        "knot_frac": jnp.clip(1.0 * jax.random.uniform(splits[3], (OBS, LANDMARKS), jnp.float32) ** level_of(splits[3], (OBS, LANDMARKS), ((1, 128),), -0.2, 0.2), 0.0, 1.0),
        "track_len": touch_ends(jax.random.randint(splits[4], (LANDMARKS,), 2, OBS + 1), jax.random.fold_in(splits[4], 1), 2, OBS).astype(jnp.int32),
        "block_base": draw_block_base(jax.random.fold_in(splits[7], 71), 0),
        "damping": jnp.clip(jnp.exp(math.log(1.5) - 2.3025851 * jax.random.uniform(splits[6], (C,), jnp.float32) ** level_of(splits[6], (C,), ((0, 4),), -0.2, 0.2)), 0.15, 1.5),
    }


def basis_weights(knot_frac):
    u = knot_frac
    u_square = u * u
    u_cubed = u_square * u
    return ((1.0 - u) ** 3 / 6.0, (3.0 * u_cubed - 6.0 * u_square + 4.0) / 6.0, (-3.0 * u_cubed + 3.0 * u_square + 3.0 * u + 1.0) / 6.0, u_cubed / 6.0)

def reduce_rows(land_jac, pose_jac, segment, knot_frac, track_len):
    num_obs = segment.shape[0]
    landmarks = segment.shape[1]
    observed = (lax.broadcasted_iota(jnp.int32, (num_obs, landmarks), 0) < track_len[None, :]).astype(jnp.float32)
    row_mask = jnp.repeat(observed, 2, axis=0)
    landmark = land_jac * row_mask[:, None, :]
    pose_rows = (pose_jac * row_mask[:, None, :]).reshape(num_obs, 2, 1, KDOF, landmarks)
    weights = basis_weights(knot_frac)
    knot_index = lax.broadcasted_iota(jnp.int32, (1, WIN_KNOTS, 1), 1)
    knot_weight = jnp.zeros((num_obs, WIN_KNOTS, landmarks), jnp.float32)
    for k in range(4):
        knot_weight = knot_weight + weights[k][:, None, :] * (segment[:, None, :] + k == knot_index).astype(jnp.float32)
    knot_jac = (knot_weight[:, None, :, None, :] * pose_rows).reshape(2 * num_obs, WIN_KNOTS * KDOF, landmarks)
    for k in range(3):
        column = landmark[k:, k, :]
        length = jnp.sqrt(lax.optimization_barrier(jnp.sum(column * column, axis=0)))
        signum = jnp.where(column[0] >= 0.0, 1.0, -1.0)
        leading = column[0] + signum * length
        vector = jnp.concatenate([leading[None, :], column[1:]], axis=0)
        reflect_scale = 2.0 / lax.optimization_barrier(jnp.sum(vector * vector, axis=0))

        def reflect(matrix):
            lower_rows = matrix[k:]
            projection = lax.optimization_barrier(jnp.sum(vector[:, None, :] * lower_rows, axis=0))
            updated = lower_rows - (reflect_scale * vector)[:, None, :] * projection[None, :, :]
            return jnp.concatenate([matrix[:k], updated], axis=0)
        landmark = reflect(landmark)
        knot_jac = reflect(knot_jac)
    return knot_jac[3:]

def block_grams(reduced, num_blocks):
    red_rows, win_width, landmarks = reduced.shape
    shaped = reduced.reshape(red_rows, win_width, num_blocks, landmarks // num_blocks)
    return jnp.einsum('rcbl,rdbl->bcd', shaped, shaped, precision=lax.Precision.HIGHEST)

def place_blocks(gram_sum, block_gram, block_start):
    win_width = block_gram.shape[1]
    group_cols = gram_sum.shape[1]
    group_knots = group_cols // KDOF

    def add_block(position, running):
        base_knot = block_start[position]
        group_id = base_knot // group_knots
        offset = base_knot % group_knots * KDOF
        row_start = (group_id * group_cols + offset).astype(jnp.int32)
        col_start = offset.astype(jnp.int32)
        current = lax.dynamic_slice(running, (row_start, col_start), (win_width, win_width))
        return lax.dynamic_update_slice(running, current + block_gram[position], (row_start, col_start))
    return lax.fori_loop(0, block_gram.shape[0], add_block, gram_sum)

def reference(land_jac, pose_jac, segment, knot_frac, track_len, block_base, damping):
    span = BLK_DEV * LBLK

    def step(position, gram_sum):
        start = (position * span).astype(jnp.int32)
        reduced = reduce_rows(lax.dynamic_slice_in_dim(land_jac, start, span, 2), lax.dynamic_slice_in_dim(pose_jac, start, span, 2), lax.dynamic_slice_in_dim(segment, start, span, 1), lax.dynamic_slice_in_dim(knot_frac, start, span, 1), lax.dynamic_slice_in_dim(track_len, start, span, 0))
        grams = block_grams(reduced, BLK_DEV)
        block_start = lax.dynamic_slice_in_dim(block_base, (position * BLK_DEV).astype(jnp.int32), BLK_DEV, 0)
        return place_blocks(gram_sum, grams, block_start)
    gram_sum = lax.fori_loop(0, BLOCKS // BLK_DEV, step, jnp.zeros((C, CG), jnp.float32))
    pieces = []
    for group_id in range(N_COLS):
        matrix = gram_sum[group_id * CG:(group_id + 1) * CG] + jnp.diag(damping[group_id * CG:(group_id + 1) * CG])
        pieces.append(jnp.linalg.cholesky(matrix).T)
    return jnp.concatenate(pieces, axis=0)
```

```python
import jax
import jax.numpy as jnp
from jax import lax
from jax.sharding import PartitionSpec as P

KDOF = 6
WIN_KNOTS = 8


def basis_weights(knot_frac):
    u_square = knot_frac * knot_frac
    u_cubed = u_square * knot_frac
    return (
        (1.0 - knot_frac) ** 3 / 6.0,
        (3.0 * u_cubed - 6.0 * u_square + 4.0) / 6.0,
        (-3.0 * u_cubed + 3.0 * u_square + 3.0 * knot_frac + 1.0) / 6.0,
        u_cubed / 6.0,
    )


def reduce_rows(land_jac, pose_jac, segment, knot_frac, track_len):
    num_obs = segment.shape[0]
    landmarks = segment.shape[1]
    observed = (
        lax.broadcasted_iota(jnp.int32, (num_obs, landmarks), 0) < track_len[None, :]
    ).astype(jnp.float32)
    row_mask = jnp.repeat(observed, 2, axis=0)
    landmark = land_jac * row_mask[:, None, :]
    pose_rows = (pose_jac * row_mask[:, None, :]).reshape(num_obs, 2, 1, KDOF, landmarks)
    weights = basis_weights(knot_frac)
    knot_index = lax.broadcasted_iota(jnp.int32, (1, WIN_KNOTS, 1), 1)
    knot_weight = jnp.zeros((num_obs, WIN_KNOTS, landmarks), jnp.float32)
    for k in range(4):
        knot_weight = knot_weight + weights[k][:, None, :] * (
            segment[:, None, :] + k == knot_index
        ).astype(jnp.float32)
    knot_jac = (knot_weight[:, None, :, None, :] * pose_rows).reshape(
        2 * num_obs, WIN_KNOTS * KDOF, landmarks
    )
    for k in range(3):
        column = landmark[k:, k, :]
        length = jnp.sqrt(jnp.sum(column * column, axis=0))
        signum = jnp.where(column[0] >= 0.0, 1.0, -1.0)
        leading = column[0] + signum * length
        vector = jnp.concatenate([leading[None, :], column[1:]], axis=0)
        reflect_scale = 2.0 / jnp.sum(vector * vector, axis=0)

        def reflect(matrix):
            lower_rows = matrix[k:]
            projection = jnp.sum(vector[:, None, :] * lower_rows, axis=0)
            updated = lower_rows - (reflect_scale * vector)[:, None, :] * projection[None, :, :]
            return jnp.concatenate([matrix[:k], updated], axis=0)

        landmark = reflect(landmark)
        knot_jac = reflect(knot_jac)
    return knot_jac[3:]


def block_grams(reduced, num_blocks):
    red_rows, win_width, landmarks = reduced.shape
    shaped = reduced.reshape(red_rows, win_width, num_blocks, landmarks // num_blocks)
    return jnp.einsum("rcbl,rdbl->bcd", shaped, shaped, precision=lax.Precision.HIGHEST)


def skew_blocks(grams):
    num_blocks = grams.shape[0]
    g5 = grams.reshape(num_blocks, WIN_KNOTS, KDOF, WIN_KNOTS, KDOF)
    k1 = lax.broadcasted_iota(jnp.int32, (WIN_KNOTS, WIN_KNOTS, WIN_KNOTS), 0)
    k2 = lax.broadcasted_iota(jnp.int32, (WIN_KNOTS, WIN_KNOTS, WIN_KNOTS), 1)
    d = lax.broadcasted_iota(jnp.int32, (WIN_KNOTS, WIN_KNOTS, WIN_KNOTS), 2)
    pick = (k2 == k1 + d).astype(jnp.float32)
    return jnp.einsum("bienf,ind->bidef", g5, pick, precision=lax.Precision.HIGHEST)


def place_band(skewed, block_start, group_cols, num_groups):
    num_blocks = skewed.shape[0]
    group_knots = group_cols // KDOF
    rows = num_groups * group_knots
    target = (block_start // group_knots) * group_knots + block_start % group_knots
    target = target[:, None] + jnp.arange(WIN_KNOTS, dtype=jnp.int32)[None, :]
    row_id = lax.broadcasted_iota(jnp.int32, (rows, num_blocks, WIN_KNOTS), 0)
    onehot = (row_id == target[None]).astype(jnp.float32).reshape(rows, num_blocks * WIN_KNOTS)
    flat = skewed.reshape(num_blocks * WIN_KNOTS, WIN_KNOTS * KDOF * KDOF)
    return jnp.dot(onehot, flat, precision=lax.Precision.HIGHEST)


def band_to_lower(band, group_cols):
    group_knots = group_cols // KDOF
    band4 = band.reshape(group_knots, WIN_KNOTS, KDOF, KDOF)
    k = lax.broadcasted_iota(jnp.int32, (group_knots, WIN_KNOTS, group_knots), 0)
    d = lax.broadcasted_iota(jnp.int32, (group_knots, WIN_KNOTS, group_knots), 1)
    m = lax.broadcasted_iota(jnp.int32, (group_knots, WIN_KNOTS, group_knots), 2)
    spread = (m == k + d).astype(jnp.float32)
    lower = jnp.einsum("kdef,kdm->mfke", band4, spread, precision=lax.Precision.HIGHEST)
    return lower.reshape(group_cols, group_cols)


def local(land_jac, pose_jac, segment, knot_frac, track_len, block_base, damping):
    num_blocks = block_base.shape[0]
    reduced = reduce_rows(land_jac, pose_jac, segment, knot_frac, track_len)
    grams = block_grams(reduced, num_blocks)
    group_cols = damping.shape[0]
    num_groups = lax.axis_size("cols")
    band = place_band(skew_blocks(grams), block_base, group_cols, num_groups)
    group_band = lax.psum_scatter(band, "cols", scatter_dimension=0, tiled=True)
    band_whole = lax.psum(group_band, "rows")
    lower = band_to_lower(band_whole, group_cols) + jnp.diag(damping)
    factors = lax.linalg.cholesky(lower, symmetrize_input=False).T
    return factors


def solution(mesh):
    return jax.shard_map(
        local,
        mesh=mesh,
        in_specs=(
            P(None, None, ("rows", "cols")),
            P(None, None, ("rows", "cols")),
            P(None, ("rows", "cols")),
            P(None, ("rows", "cols")),
            P(("rows", "cols")),
            P(("rows", "cols")),
            P("cols"),
        ),
        out_specs=P("cols", None),
        check_vma=False,
    )
```

```python
import jax
import jax.numpy as jnp
from jax import lax
from jax.sharding import PartitionSpec as P

KDOF = 6
WIN_KNOTS = 8


def basis_weights(knot_frac):
    u_square = knot_frac * knot_frac
    u_cubed = u_square * knot_frac
    return (
        (1.0 - knot_frac) ** 3 / 6.0,
        (3.0 * u_cubed - 6.0 * u_square + 4.0) / 6.0,
        (-3.0 * u_cubed + 3.0 * u_square + 3.0 * knot_frac + 1.0) / 6.0,
        u_cubed / 6.0,
    )


def reduce_rows(land_jac, pose_jac, segment, knot_frac, track_len):
    num_obs = segment.shape[0]
    landmarks = segment.shape[1]
    observed = (
        lax.broadcasted_iota(jnp.int32, (num_obs, landmarks), 0) < track_len[None, :]
    ).astype(jnp.float32)
    row_mask = jnp.repeat(observed, 2, axis=0)
    landmark = land_jac * row_mask[:, None, :]
    pose_rows = (pose_jac * row_mask[:, None, :]).reshape(num_obs, 2, 1, KDOF, landmarks)
    weights = basis_weights(knot_frac)
    knot_index = lax.broadcasted_iota(jnp.int32, (1, WIN_KNOTS, 1), 1)
    knot_weight = jnp.zeros((num_obs, WIN_KNOTS, landmarks), jnp.float32)
    for k in range(4):
        knot_weight = knot_weight + weights[k][:, None, :] * (
            segment[:, None, :] + k == knot_index
        ).astype(jnp.float32)
    knot_jac = (knot_weight[:, None, :, None, :] * pose_rows).reshape(
        2 * num_obs, WIN_KNOTS * KDOF, landmarks
    )
    for k in range(3):
        column = landmark[k:, k, :]
        length = jnp.sqrt(jnp.sum(column * column, axis=0))
        signum = jnp.where(column[0] >= 0.0, 1.0, -1.0)
        leading = column[0] + signum * length
        vector = jnp.concatenate([leading[None, :], column[1:]], axis=0)
        reflect_scale = 2.0 / jnp.sum(vector * vector, axis=0)

        def reflect(matrix):
            lower_rows = matrix[k:]
            projection = jnp.sum(vector[:, None, :] * lower_rows, axis=0)
            updated = lower_rows - (reflect_scale * vector)[:, None, :] * projection[None, :, :]
            return jnp.concatenate([matrix[:k], updated], axis=0)

        landmark = reflect(landmark)
        knot_jac = reflect(knot_jac)
    return knot_jac[3:]


def block_grams(reduced, num_blocks):
    red_rows, win_width, landmarks = reduced.shape
    shaped = reduced.reshape(red_rows, win_width, num_blocks, landmarks // num_blocks)
    return jnp.einsum("rcbl,rdbl->bcd", shaped, shaped, precision=lax.Precision.HIGHEST)


def skew_blocks(grams):
    num_blocks = grams.shape[0]
    g5 = grams.reshape(num_blocks, WIN_KNOTS, KDOF, WIN_KNOTS, KDOF)
    k1 = lax.broadcasted_iota(jnp.int32, (WIN_KNOTS, WIN_KNOTS, WIN_KNOTS), 0)
    k2 = lax.broadcasted_iota(jnp.int32, (WIN_KNOTS, WIN_KNOTS, WIN_KNOTS), 1)
    d = lax.broadcasted_iota(jnp.int32, (WIN_KNOTS, WIN_KNOTS, WIN_KNOTS), 2)
    pick = (k2 == k1 + d).astype(jnp.float32)
    return jnp.einsum("bienf,ind->bidef", g5, pick, precision=lax.Precision.HIGHEST)


def place_band(skewed, block_start, group_cols, num_groups):
    num_blocks = skewed.shape[0]
    group_knots = group_cols // KDOF
    rows = num_groups * group_knots
    target = (block_start // group_knots) * group_knots + block_start % group_knots
    target = target[:, None] + jnp.arange(WIN_KNOTS, dtype=jnp.int32)[None, :]
    row_id = lax.broadcasted_iota(jnp.int32, (rows, num_blocks, WIN_KNOTS), 0)
    onehot = (row_id == target[None]).astype(jnp.float32).reshape(rows, num_blocks * WIN_KNOTS)
    flat = skewed.reshape(num_blocks * WIN_KNOTS, WIN_KNOTS * KDOF * KDOF)
    return jnp.dot(onehot, flat, precision=lax.Precision.HIGHEST)


def band_to_lower(band, group_cols):
    group_knots = group_cols // KDOF
    band4 = band.reshape(group_knots, WIN_KNOTS, KDOF, KDOF)
    k = lax.broadcasted_iota(jnp.int32, (group_knots, WIN_KNOTS, group_knots), 0)
    d = lax.broadcasted_iota(jnp.int32, (group_knots, WIN_KNOTS, group_knots), 1)
    m = lax.broadcasted_iota(jnp.int32, (group_knots, WIN_KNOTS, group_knots), 2)
    spread = (m == k + d).astype(jnp.float32)
    lower = jnp.einsum("kdef,kdm->mfke", band4, spread, precision=lax.Precision.HIGHEST)
    return lower.reshape(group_cols, group_cols)


def halve_over(band, axis):
    n = lax.axis_size(axis)
    c = lax.axis_index(axis)
    size = band.shape[0]
    s = n // 2
    while s >= 1:
        half = size // 2
        bit = (c // s) % 2
        keep = lax.dynamic_slice_in_dim(band, bit * half, half, 0)
        send = lax.dynamic_slice_in_dim(band, (1 - bit) * half, half, 0)
        band = keep + lax.ppermute(send, axis, [(i, i ^ s) for i in range(n)])
        size = half
        s //= 2
    return band


def butterfly_sum(band, axis):
    n = lax.axis_size(axis)
    s = 1
    while s < n:
        band = band + lax.ppermute(band, axis, [(i, i ^ s) for i in range(n)])
        s *= 2
    return band


def local(land_jac, pose_jac, segment, knot_frac, track_len, block_base, damping):
    num_blocks = block_base.shape[0]
    reduced = reduce_rows(land_jac, pose_jac, segment, knot_frac, track_len)
    grams = block_grams(reduced, num_blocks)
    group_cols = damping.shape[0]
    num_groups = lax.axis_size("cols")
    band = place_band(skew_blocks(grams), block_base, group_cols, num_groups)
    band_whole = butterfly_sum(halve_over(band, "cols"), "rows")
    lower = band_to_lower(band_whole, group_cols) + jnp.diag(damping)
    factors = lax.linalg.cholesky(lower, symmetrize_input=False).T
    return factors


def solution(mesh):
    return jax.shard_map(
        local,
        mesh=mesh,
        in_specs=(
            P(None, None, ("rows", "cols")),
            P(None, None, ("rows", "cols")),
            P(None, ("rows", "cols")),
            P(None, ("rows", "cols")),
            P(("rows", "cols")),
            P(("rows", "cols")),
            P("cols"),
        ),
        out_specs=P("cols", None),
        check_vma=False,
    )
```

```python
import jax
import jax.numpy as jnp
from jax import lax
from jax.sharding import PartitionSpec as P
from jax.experimental import pallas as pl
from jax.experimental.pallas import tpu as pltpu
import functools

KDOF = 6
WIN_KNOTS = 8
PANEL = 8
WIDTH = 256


def basis_weights(knot_frac):
    u_square = knot_frac * knot_frac
    u_cubed = u_square * knot_frac
    return (
        (1.0 - knot_frac) ** 3 / 6.0,
        (3.0 * u_cubed - 6.0 * u_square + 4.0) / 6.0,
        (-3.0 * u_cubed + 3.0 * u_square + 3.0 * knot_frac + 1.0) / 6.0,
        u_cubed / 6.0,
    )


def reduce_rows(land_jac, pose_jac, segment, knot_frac, track_len):
    num_obs = segment.shape[0]
    landmarks = segment.shape[1]
    observed = (
        lax.broadcasted_iota(jnp.int32, (num_obs, landmarks), 0) < track_len[None, :]
    ).astype(jnp.float32)
    row_mask = jnp.repeat(observed, 2, axis=0)
    landmark = land_jac * row_mask[:, None, :]
    pose_rows = (pose_jac * row_mask[:, None, :]).reshape(num_obs, 2, 1, KDOF, landmarks)
    weights = basis_weights(knot_frac)
    knot_index = lax.broadcasted_iota(jnp.int32, (1, WIN_KNOTS, 1), 1)
    knot_weight = jnp.zeros((num_obs, WIN_KNOTS, landmarks), jnp.float32)
    for k in range(4):
        knot_weight = knot_weight + weights[k][:, None, :] * (
            segment[:, None, :] + k == knot_index
        ).astype(jnp.float32)
    knot_jac = (knot_weight[:, None, :, None, :] * pose_rows).reshape(
        2 * num_obs, WIN_KNOTS * KDOF, landmarks
    )
    for k in range(3):
        column = landmark[k:, k, :]
        length = jnp.sqrt(jnp.sum(column * column, axis=0))
        signum = jnp.where(column[0] >= 0.0, 1.0, -1.0)
        leading = column[0] + signum * length
        vector = jnp.concatenate([leading[None, :], column[1:]], axis=0)
        reflect_scale = 2.0 / jnp.sum(vector * vector, axis=0)

        def reflect(matrix):
            lower_rows = matrix[k:]
            projection = jnp.sum(vector[:, None, :] * lower_rows, axis=0)
            updated = lower_rows - (reflect_scale * vector)[:, None, :] * projection[None, :, :]
            return jnp.concatenate([matrix[:k], updated], axis=0)

        landmark = reflect(landmark)
        knot_jac = reflect(knot_jac)
    return knot_jac[3:]


def block_grams(reduced, num_blocks):
    red_rows, win_width, landmarks = reduced.shape
    shaped = reduced.reshape(red_rows, win_width, num_blocks, landmarks // num_blocks)
    return jnp.einsum("rcbl,rdbl->bcd", shaped, shaped, precision=lax.Precision.HIGHEST)


def skew_blocks(grams):
    num_blocks = grams.shape[0]
    g5 = grams.reshape(num_blocks, WIN_KNOTS, KDOF, WIN_KNOTS, KDOF)
    k1 = lax.broadcasted_iota(jnp.int32, (WIN_KNOTS, WIN_KNOTS, WIN_KNOTS), 0)
    k2 = lax.broadcasted_iota(jnp.int32, (WIN_KNOTS, WIN_KNOTS, WIN_KNOTS), 1)
    d = lax.broadcasted_iota(jnp.int32, (WIN_KNOTS, WIN_KNOTS, WIN_KNOTS), 2)
    pick = (k2 == k1 + d).astype(jnp.float32)
    return jnp.einsum("bienf,ind->bidef", g5, pick, precision=lax.Precision.HIGHEST)


def place_band(skewed, block_start, group_cols, num_groups):
    num_blocks = skewed.shape[0]
    group_knots = group_cols // KDOF
    rows = num_groups * group_knots
    target = (block_start // group_knots) * group_knots + block_start % group_knots
    target = target[:, None] + jnp.arange(WIN_KNOTS, dtype=jnp.int32)[None, :]
    row_id = lax.broadcasted_iota(jnp.int32, (rows, num_blocks, WIN_KNOTS), 0)
    onehot = (row_id == target[None]).astype(jnp.float32).reshape(rows, num_blocks * WIN_KNOTS)
    flat = skewed.reshape(num_blocks * WIN_KNOTS, WIN_KNOTS * KDOF * KDOF)
    return jnp.dot(onehot, flat, precision=lax.Precision.HIGHEST)


def band_to_lower(band, group_cols):
    group_knots = group_cols // KDOF
    band4 = band.reshape(group_knots, WIN_KNOTS, KDOF, KDOF)
    k = lax.broadcasted_iota(jnp.int32, (group_knots, WIN_KNOTS, group_knots), 0)
    d = lax.broadcasted_iota(jnp.int32, (group_knots, WIN_KNOTS, group_knots), 1)
    m = lax.broadcasted_iota(jnp.int32, (group_knots, WIN_KNOTS, group_knots), 2)
    spread = (m == k + d).astype(jnp.float32)
    lower = jnp.einsum("kdef,kdm->mfke", band4, spread, precision=lax.Precision.HIGHEST)
    return lower.reshape(group_cols, group_cols)


def band_chol_kernel(n, band_w, yt_ref, out_ref, w_ref, r_ref, u_ref):
    w_ref[...] = jnp.zeros_like(w_ref)
    r_ref[...] = jnp.zeros_like(r_ref)
    lanes = lax.broadcasted_iota(jnp.int32, (band_w, WIDTH), 1)
    for k in range(n // KDOF):
        lo = KDOF * k
        tile = (lo // 128) * 128
        blk = yt_ref[:, tile:tile + WIDTH]
        keep = (lanes >= lo - tile) & (lanes < lo - tile + KDOF)
        w_ref[lo:lo + band_w, tile:tile + WIDTH] += jnp.where(keep, blk, 0.0)
    tiles = n // 128
    ri = lax.broadcasted_iota(jnp.int32, (128, 128), 0)
    ci = lax.broadcasted_iota(jnp.int32, (128, 128), 1)
    for a in range(tiles):
        for b in (a, a + 1):
            if b >= tiles:
                continue
            low = w_ref[128 * a:128 * a + 128, 128 * b:128 * b + 128]
            mirror = w_ref[128 * b:128 * b + 128, 128 * a:128 * a + 128].T
            upper = (ci + 128 * b) // KDOF > (ri + 128 * a) // KDOF
            w_ref[128 * a:128 * a + 128, 128 * b:128 * b + 128] = jnp.where(upper, mirror, low)

    lane = lax.broadcasted_iota(jnp.int32, (PANEL, WIDTH), 1)
    row = lax.broadcasted_iota(jnp.int32, (PANEL, 1), 0)

    def panel(p, carry):
        j0 = pl.multiple_of(p * PANEL, PANEL)
        base = pl.multiple_of((p // (128 // PANEL)) * 128, 128)
        off = j0 - base
        blk = w_ref[pl.ds(j0, PANEL), pl.ds(base, WIDTH)]
        out_rows = []
        for t in range(PANEL):
            jt = off + t
            col = jnp.sum(jnp.where(lane == jt, blk, 0.0), axis=1, keepdims=True)
            inv = lax.rsqrt(col[t:t + 1, :])
            rrow = jnp.where(lane[0:1, :] >= jt, blk[t:t + 1, :] * inv, 0.0)
            out_rows.append(rrow)
            mult = jnp.where(row > t, col * inv, 0.0)
            blk = blk - mult * rrow
        rp = jnp.concatenate(out_rows, axis=0)
        r_ref[pl.ds(j0, PANEL), pl.ds(base, WIDTH)] = rp
        u_ref[...] = jnp.dot(rp.T, rp, precision=lax.Precision.HIGHEST, preferred_element_type=jnp.float32)
        start = pl.multiple_of(j0 + PANEL, PANEL)
        trail = w_ref[pl.ds(start, band_w), pl.ds(base, WIDTH)]
        w_ref[pl.ds(start, band_w), pl.ds(base, WIDTH)] = trail - u_ref[pl.ds(off + PANEL, band_w), :]
        return carry

    lax.fori_loop(0, n // PANEL, panel, 0)
    out_ref[...] = r_ref[0:n, 0:n]


def band_cholesky(yt, n):
    band_w = yt.shape[0]
    padded = n + 128
    yt = jnp.pad(yt, ((0, 0), (0, padded - n)))
    return pl.pallas_call(
        functools.partial(band_chol_kernel, n, band_w),
        out_shape=jax.ShapeDtypeStruct((n, n), jnp.float32),
        in_specs=[pl.BlockSpec(memory_space=pltpu.VMEM)],
        out_specs=pl.BlockSpec(memory_space=pltpu.VMEM),
        scratch_shapes=[
            pltpu.VMEM((n + 64, padded), jnp.float32),
            pltpu.VMEM((n, padded), jnp.float32),
            pltpu.VMEM((WIDTH, WIDTH), jnp.float32),
        ],
    )(yt)


def halve_over(band, axis):
    n = lax.axis_size(axis)
    c = lax.axis_index(axis)
    size = band.shape[0]
    s = n // 2
    while s >= 1:
        half = size // 2
        bit = (c // s) % 2
        keep = lax.dynamic_slice_in_dim(band, bit * half, half, 0)
        send = lax.dynamic_slice_in_dim(band, (1 - bit) * half, half, 0)
        band = keep + lax.ppermute(send, axis, [(i, i ^ s) for i in range(n)])
        size = half
        s //= 2
    return band


def butterfly_sum(band, axis):
    n = lax.axis_size(axis)
    s = 1
    while s < n:
        band = band + lax.ppermute(band, axis, [(i, i ^ s) for i in range(n)])
        s *= 2
    return band


def local(land_jac, pose_jac, segment, knot_frac, track_len, block_base, damping):
    num_blocks = block_base.shape[0]
    reduced = reduce_rows(land_jac, pose_jac, segment, knot_frac, track_len)
    grams = block_grams(reduced, num_blocks)
    group_cols = damping.shape[0]
    num_groups = lax.axis_size("cols")
    band = place_band(skew_blocks(grams), block_base, group_cols, num_groups)
    band_whole = butterfly_sum(halve_over(band, "cols"), "rows")
    group_knots = group_cols // KDOF
    yt = band_whole.reshape(group_knots, WIN_KNOTS, KDOF, KDOF).transpose(1, 3, 0, 2)
    yt = yt.reshape(WIN_KNOTS * KDOF, group_cols)
    t = lax.broadcasted_iota(jnp.int32, yt.shape, 0)
    i = lax.broadcasted_iota(jnp.int32, yt.shape, 1)
    yt = yt + jnp.where(t == i % KDOF, damping[None, :], 0.0)
    return band_cholesky(yt, group_cols)


def solution(mesh):
    return jax.shard_map(
        local,
        mesh=mesh,
        in_specs=(
            P(None, None, ("rows", "cols")),
            P(None, None, ("rows", "cols")),
            P(None, ("rows", "cols")),
            P(None, ("rows", "cols")),
            P(("rows", "cols")),
            P(("rows", "cols")),
            P("cols"),
        ),
        out_specs=P("cols", None),
        check_vma=False,
    )
```

```python
import jax
import jax.numpy as jnp
from jax import lax
from jax.sharding import PartitionSpec as P
from jax.experimental import pallas as pl
from jax.experimental.pallas import tpu as pltpu
import functools

KDOF = 6
WIN_KNOTS = 8
PANEL = 8
WIDTH = 256


def basis_weights(knot_frac):
    u_square = knot_frac * knot_frac
    u_cubed = u_square * knot_frac
    return (
        (1.0 - knot_frac) ** 3 / 6.0,
        (3.0 * u_cubed - 6.0 * u_square + 4.0) / 6.0,
        (-3.0 * u_cubed + 3.0 * u_square + 3.0 * knot_frac + 1.0) / 6.0,
        u_cubed / 6.0,
    )


def reduce_rows(land_jac, pose_jac, segment, knot_frac, track_len):
    num_obs = segment.shape[0]
    landmarks = segment.shape[1]
    observed = (
        lax.broadcasted_iota(jnp.int32, (num_obs, landmarks), 0) < track_len[None, :]
    ).astype(jnp.float32)
    row_mask = jnp.repeat(observed, 2, axis=0)
    landmark = land_jac * row_mask[:, None, :]
    pose_rows = (pose_jac * row_mask[:, None, :]).reshape(num_obs, 2, 1, KDOF, landmarks)
    weights = basis_weights(knot_frac)
    knot_index = lax.broadcasted_iota(jnp.int32, (1, WIN_KNOTS, 1), 1)
    knot_weight = jnp.zeros((num_obs, WIN_KNOTS, landmarks), jnp.float32)
    for k in range(4):
        knot_weight = knot_weight + weights[k][:, None, :] * (
            segment[:, None, :] + k == knot_index
        ).astype(jnp.float32)
    knot_jac = (knot_weight[:, None, :, None, :] * pose_rows).reshape(
        2 * num_obs, WIN_KNOTS * KDOF, landmarks
    )
    for k in range(3):
        column = landmark[k:, k, :]
        length = jnp.sqrt(jnp.sum(column * column, axis=0))
        signum = jnp.where(column[0] >= 0.0, 1.0, -1.0)
        leading = column[0] + signum * length
        vector = jnp.concatenate([leading[None, :], column[1:]], axis=0)
        reflect_scale = 2.0 / jnp.sum(vector * vector, axis=0)

        def reflect(matrix):
            lower_rows = matrix[k:]
            projection = jnp.sum(vector[:, None, :] * lower_rows, axis=0)
            updated = lower_rows - (reflect_scale * vector)[:, None, :] * projection[None, :, :]
            return jnp.concatenate([matrix[:k], updated], axis=0)

        landmark = reflect(landmark)
        knot_jac = reflect(knot_jac)
    return knot_jac[3:]


def block_grams(reduced, num_blocks):
    red_rows, win_width, landmarks = reduced.shape
    shaped = reduced.reshape(red_rows, win_width, num_blocks, landmarks // num_blocks)
    return jnp.einsum("rcbl,rdbl->bcd", shaped, shaped, precision=lax.Precision.HIGHEST)


def skew_blocks(grams):
    num_blocks = grams.shape[0]
    g5 = grams.reshape(num_blocks, WIN_KNOTS, KDOF, WIN_KNOTS, KDOF)
    k1 = lax.broadcasted_iota(jnp.int32, (WIN_KNOTS, WIN_KNOTS, WIN_KNOTS), 0)
    k2 = lax.broadcasted_iota(jnp.int32, (WIN_KNOTS, WIN_KNOTS, WIN_KNOTS), 1)
    d = lax.broadcasted_iota(jnp.int32, (WIN_KNOTS, WIN_KNOTS, WIN_KNOTS), 2)
    pick = (k2 == k1 + d).astype(jnp.float32)
    return jnp.einsum("bienf,ind->bidef", g5, pick, precision=lax.Precision.HIGHEST)


def place_band(skewed, block_start, group_cols, num_groups):
    num_blocks = skewed.shape[0]
    group_knots = group_cols // KDOF
    rows = num_groups * group_knots
    target = (block_start // group_knots) * group_knots + block_start % group_knots
    target = target[:, None] + jnp.arange(WIN_KNOTS, dtype=jnp.int32)[None, :]
    row_id = lax.broadcasted_iota(jnp.int32, (rows, num_blocks, WIN_KNOTS), 0)
    onehot = (row_id == target[None]).astype(jnp.float32).reshape(rows, num_blocks * WIN_KNOTS)
    flat = skewed.reshape(num_blocks * WIN_KNOTS, WIN_KNOTS * KDOF * KDOF)
    return jnp.dot(onehot, flat, precision=lax.Precision.HIGHEST)


def band_chol_kernel(n, band_w, yt_ref, out_ref, w_ref, r_ref):
    w_ref[...] = jnp.zeros_like(w_ref)
    r_ref[...] = jnp.zeros_like(r_ref)
    lanes = lax.broadcasted_iota(jnp.int32, (band_w, WIDTH), 1)
    for k in range(n // KDOF):
        lo = KDOF * k
        tile = (lo // 128) * 128
        blk = yt_ref[:, tile:tile + WIDTH]
        keep = (lanes >= lo - tile) & (lanes < lo - tile + KDOF)
        w_ref[lo:lo + band_w, tile:tile + WIDTH] += jnp.where(keep, blk, 0.0)
    tiles = n // 128
    ri = lax.broadcasted_iota(jnp.int32, (128, 128), 0)
    ci = lax.broadcasted_iota(jnp.int32, (128, 128), 1)
    for a in range(tiles):
        for b in (a, a + 1):
            if b >= tiles:
                continue
            low = w_ref[128 * a:128 * a + 128, 128 * b:128 * b + 128]
            mirror = w_ref[128 * b:128 * b + 128, 128 * a:128 * a + 128].T
            upper = (ci + 128 * b) // KDOF > (ri + 128 * a) // KDOF
            w_ref[128 * a:128 * a + 128, 128 * b:128 * b + 128] = jnp.where(upper, mirror, low)

    rows = PANEL + band_w
    lane = lax.broadcasted_iota(jnp.int32, (rows, WIDTH), 1)
    row = lax.broadcasted_iota(jnp.int32, (rows, 1), 0)

    def panel(p, carry):
        j0 = pl.multiple_of(p * PANEL, PANEL)
        base = pl.multiple_of((p // (128 // PANEL)) * 128, 128)
        off = j0 - base
        blk = w_ref[pl.ds(j0, rows), pl.ds(base, WIDTH)]
        out_rows = []
        for t in range(PANEL):
            jt = off + t
            col = jnp.sum(jnp.where(lane == jt, blk, 0.0), axis=1, keepdims=True)
            inv = lax.rsqrt(col[t:t + 1, :])
            rrow = jnp.where(lane[0:1, :] >= jt, blk[t:t + 1, :] * inv, 0.0)
            out_rows.append(rrow)
            mult = jnp.where(row > t, col * inv, 0.0)
            blk = blk - mult * rrow
        r_ref[pl.ds(j0, PANEL), pl.ds(base, WIDTH)] = jnp.concatenate(out_rows, axis=0)
        start = pl.multiple_of(j0 + PANEL, PANEL)
        w_ref[pl.ds(start, band_w), pl.ds(base, WIDTH)] = blk[PANEL:, :]
        return carry

    lax.fori_loop(0, n // PANEL, panel, 0)
    out_ref[...] = r_ref[0:n, 0:n]


def band_cholesky(yt, n):
    band_w = yt.shape[0]
    padded = n + 128
    yt = jnp.pad(yt, ((0, 0), (0, padded - n)))
    return pl.pallas_call(
        functools.partial(band_chol_kernel, n, band_w),
        out_shape=jax.ShapeDtypeStruct((n, n), jnp.float32),
        in_specs=[pl.BlockSpec(memory_space=pltpu.VMEM)],
        out_specs=pl.BlockSpec(memory_space=pltpu.VMEM),
        scratch_shapes=[
            pltpu.VMEM((n + 64, padded), jnp.float32),
            pltpu.VMEM((n, padded), jnp.float32),
        ],
    )(yt)


def halve_over(band, axis):
    n = lax.axis_size(axis)
    c = lax.axis_index(axis)
    size = band.shape[0]
    s = n // 2
    while s >= 1:
        half = size // 2
        bit = (c // s) % 2
        keep = lax.dynamic_slice_in_dim(band, bit * half, half, 0)
        send = lax.dynamic_slice_in_dim(band, (1 - bit) * half, half, 0)
        band = keep + lax.ppermute(send, axis, [(i, i ^ s) for i in range(n)])
        size = half
        s //= 2
    return band


def butterfly_sum(band, axis):
    n = lax.axis_size(axis)
    s = 1
    while s < n:
        band = band + lax.ppermute(band, axis, [(i, i ^ s) for i in range(n)])
        s *= 2
    return band


def local(land_jac, pose_jac, segment, knot_frac, track_len, block_base, damping):
    num_blocks = block_base.shape[0]
    reduced = reduce_rows(land_jac, pose_jac, segment, knot_frac, track_len)
    grams = block_grams(reduced, num_blocks)
    group_cols = damping.shape[0]
    num_groups = lax.axis_size("cols")
    band = place_band(skew_blocks(grams), block_base, group_cols, num_groups)
    band_whole = butterfly_sum(halve_over(band, "cols"), "rows")
    group_knots = group_cols // KDOF
    yt = band_whole.reshape(group_knots, WIN_KNOTS, KDOF, KDOF).transpose(1, 3, 0, 2)
    yt = yt.reshape(WIN_KNOTS * KDOF, group_cols)
    t = lax.broadcasted_iota(jnp.int32, yt.shape, 0)
    i = lax.broadcasted_iota(jnp.int32, yt.shape, 1)
    yt = yt + jnp.where(t == i % KDOF, damping[None, :], 0.0)
    return band_cholesky(yt, group_cols)


def solution(mesh):
    return jax.shard_map(
        local,
        mesh=mesh,
        in_specs=(
            P(None, None, ("rows", "cols")),
            P(None, None, ("rows", "cols")),
            P(None, ("rows", "cols")),
            P(None, ("rows", "cols")),
            P(("rows", "cols")),
            P(("rows", "cols")),
            P("cols"),
        ),
        out_specs=P("cols", None),
        check_vma=False,
    )
```

```python
import jax
import jax.numpy as jnp
from jax import lax
from jax.sharding import PartitionSpec as P
from jax.experimental import pallas as pl
from jax.experimental.pallas import tpu as pltpu
import functools

KDOF = 6
WIN_KNOTS = 8
PANEL = 8
WIDTH = 256


def gram_kernel(land_ref, pose_ref, seg_ref, frac_ref, len_ref, out_ref):
    num_obs, lanes = seg_ref.shape
    rows = 2 * num_obs
    u = frac_ref[...]
    u_square = u * u
    u_cubed = u_square * u
    basis = (
        (1.0 - u) ** 3 / 6.0,
        (3.0 * u_cubed - 6.0 * u_square + 4.0) / 6.0,
        (-3.0 * u_cubed + 3.0 * u_square + 3.0 * u + 1.0) / 6.0,
        u_cubed / 6.0,
    )
    seg = seg_ref[...]
    obs = lax.broadcasted_iota(jnp.int32, (num_obs, lanes), 0)
    observed = (obs < len_ref[...]).astype(jnp.float32)
    knot = lax.broadcasted_iota(jnp.int32, (WIN_KNOTS, lanes), 0)
    land = []
    knots = []
    for j in range(num_obs):
        seg_j = seg[j:j + 1, :]
        weight = jnp.zeros((WIN_KNOTS, lanes), jnp.float32)
        for k in range(4):
            weight = weight + basis[k][j:j + 1, :] * (seg_j + k == knot).astype(jnp.float32)
        mask = observed[j:j + 1, :]
        for i in range(2):
            r = 2 * j + i
            land.append(land_ref[r] * mask)
            pose = pose_ref[r] * mask
            knots.append(jnp.concatenate([pose[e:e + 1, :] * weight for e in range(KDOF)], axis=0))
    for k in range(3):
        column = [land[r][k:k + 1, :] for r in range(k, rows)]
        total = column[0] * column[0]
        for x in column[1:]:
            total = total + x * x
        length = jnp.sqrt(total)
        signum = jnp.where(column[0] >= 0.0, 1.0, -1.0)
        vector = [column[0] + signum * length] + column[1:]
        vv = vector[0] * vector[0]
        for x in vector[1:]:
            vv = vv + x * x
        scale = 2.0 / vv
        for mats in (land, knots):
            proj = vector[0] * mats[k]
            for idx in range(1, rows - k):
                proj = proj + vector[idx] * mats[k + idx]
            for idx in range(rows - k):
                mats[k + idx] = mats[k + idx] - (scale * vector[idx]) * proj
    reduced = jnp.concatenate(knots[3:], axis=1)
    out_ref[0] = lax.dot_general(reduced, reduced, (((1,), (1,)), ((), ())),
                                 precision=lax.Precision.HIGHEST, preferred_element_type=jnp.float32)


def block_grams_kernel(land_jac, pose_jac, segment, knot_frac, track_len, num_blocks):
    rows, ldim, landmarks = land_jac.shape
    pdim = pose_jac.shape[1]
    num_obs = segment.shape[0]
    blk = landmarks // num_blocks
    width = WIN_KNOTS * KDOF
    return pl.pallas_call(
        gram_kernel,
        out_shape=jax.ShapeDtypeStruct((num_blocks, width, width), jnp.float32),
        grid=(num_blocks,),
        in_specs=[
            pl.BlockSpec((rows, ldim, blk), lambda b: (0, 0, b)),
            pl.BlockSpec((rows, pdim, blk), lambda b: (0, 0, b)),
            pl.BlockSpec((num_obs, blk), lambda b: (0, b)),
            pl.BlockSpec((num_obs, blk), lambda b: (0, b)),
            pl.BlockSpec((1, blk), lambda b: (0, b)),
        ],
        out_specs=pl.BlockSpec((1, width, width), lambda b: (b, 0, 0)),
    )(land_jac, pose_jac, segment, knot_frac, track_len.reshape(1, landmarks))


def skew_blocks(grams):
    num_blocks = grams.shape[0]
    g5 = grams.reshape(num_blocks, KDOF, WIN_KNOTS, KDOF, WIN_KNOTS).transpose(0, 2, 1, 4, 3)
    k1 = lax.broadcasted_iota(jnp.int32, (WIN_KNOTS, WIN_KNOTS, WIN_KNOTS), 0)
    k2 = lax.broadcasted_iota(jnp.int32, (WIN_KNOTS, WIN_KNOTS, WIN_KNOTS), 1)
    d = lax.broadcasted_iota(jnp.int32, (WIN_KNOTS, WIN_KNOTS, WIN_KNOTS), 2)
    pick = (k2 == k1 + d).astype(jnp.float32)
    return jnp.einsum("bienf,ind->bidef", g5, pick, precision=lax.Precision.HIGHEST)


def place_band(skewed, block_start, group_cols, num_groups):
    num_blocks = skewed.shape[0]
    group_knots = group_cols // KDOF
    rows = num_groups * group_knots
    target = (block_start // group_knots) * group_knots + block_start % group_knots
    target = target[:, None] + jnp.arange(WIN_KNOTS, dtype=jnp.int32)[None, :]
    row_id = lax.broadcasted_iota(jnp.int32, (rows, num_blocks, WIN_KNOTS), 0)
    onehot = (row_id == target[None]).astype(jnp.float32).reshape(rows, num_blocks * WIN_KNOTS)
    flat = skewed.reshape(num_blocks * WIN_KNOTS, WIN_KNOTS * KDOF * KDOF)
    return jnp.dot(onehot, flat, precision=lax.Precision.HIGHEST)


def band_chol_kernel(n, band_w, yt_ref, out_ref, w_ref, r_ref):
    w_ref[...] = jnp.zeros_like(w_ref)
    r_ref[...] = jnp.zeros_like(r_ref)
    lanes = lax.broadcasted_iota(jnp.int32, (band_w, WIDTH), 1)
    for k in range(n // KDOF):
        lo = KDOF * k
        tile = (lo // 128) * 128
        blk = yt_ref[:, tile:tile + WIDTH]
        keep = (lanes >= lo - tile) & (lanes < lo - tile + KDOF)
        w_ref[lo:lo + band_w, tile:tile + WIDTH] += jnp.where(keep, blk, 0.0)
    tiles = n // 128
    ri = lax.broadcasted_iota(jnp.int32, (128, 128), 0)
    ci = lax.broadcasted_iota(jnp.int32, (128, 128), 1)
    for a in range(tiles):
        for b in (a, a + 1):
            if b >= tiles:
                continue
            low = w_ref[128 * a:128 * a + 128, 128 * b:128 * b + 128]
            mirror = w_ref[128 * b:128 * b + 128, 128 * a:128 * a + 128].T
            upper = (ci + 128 * b) // KDOF > (ri + 128 * a) // KDOF
            w_ref[128 * a:128 * a + 128, 128 * b:128 * b + 128] = jnp.where(upper, mirror, low)

    rows = PANEL + band_w
    lane = lax.broadcasted_iota(jnp.int32, (rows, WIDTH), 1)
    row = lax.broadcasted_iota(jnp.int32, (rows, 1), 0)

    def panel(p, carry):
        j0 = pl.multiple_of(p * PANEL, PANEL)
        base = pl.multiple_of((p // (128 // PANEL)) * 128, 128)
        off = j0 - base
        blk = w_ref[pl.ds(j0, rows), pl.ds(base, WIDTH)]
        out_rows = []
        for t in range(PANEL):
            jt = off + t
            col = jnp.sum(jnp.where(lane == jt, blk, 0.0), axis=1, keepdims=True)
            inv = lax.rsqrt(col[t:t + 1, :])
            rrow = jnp.where(lane[0:1, :] >= jt, blk[t:t + 1, :] * inv, 0.0)
            out_rows.append(rrow)
            mult = jnp.where(row > t, col * inv, 0.0)
            blk = blk - mult * rrow
        r_ref[pl.ds(j0, PANEL), pl.ds(base, WIDTH)] = jnp.concatenate(out_rows, axis=0)
        start = pl.multiple_of(j0 + PANEL, PANEL)
        w_ref[pl.ds(start, band_w), pl.ds(base, WIDTH)] = blk[PANEL:, :]
        return carry

    lax.fori_loop(0, n // PANEL, panel, 0)
    out_ref[...] = r_ref[0:n, 0:n]


def band_cholesky(yt, n):
    band_w = yt.shape[0]
    padded = n + 128
    yt = jnp.pad(yt, ((0, 0), (0, padded - n)))
    return pl.pallas_call(
        functools.partial(band_chol_kernel, n, band_w),
        out_shape=jax.ShapeDtypeStruct((n, n), jnp.float32),
        in_specs=[pl.BlockSpec(memory_space=pltpu.VMEM)],
        out_specs=pl.BlockSpec(memory_space=pltpu.VMEM),
        scratch_shapes=[
            pltpu.VMEM((n + 64, padded), jnp.float32),
            pltpu.VMEM((n, padded), jnp.float32),
        ],
    )(yt)


def halve_over(band, axis):
    n = lax.axis_size(axis)
    c = lax.axis_index(axis)
    size = band.shape[0]
    s = n // 2
    while s >= 1:
        half = size // 2
        bit = (c // s) % 2
        keep = lax.dynamic_slice_in_dim(band, bit * half, half, 0)
        send = lax.dynamic_slice_in_dim(band, (1 - bit) * half, half, 0)
        band = keep + lax.ppermute(send, axis, [(i, i ^ s) for i in range(n)])
        size = half
        s //= 2
    return band


def butterfly_sum(band, axis):
    n = lax.axis_size(axis)
    s = 1
    while s < n:
        band = band + lax.ppermute(band, axis, [(i, i ^ s) for i in range(n)])
        s *= 2
    return band


def local(land_jac, pose_jac, segment, knot_frac, track_len, block_base, damping):
    num_blocks = block_base.shape[0]
    grams = block_grams_kernel(land_jac, pose_jac, segment, knot_frac, track_len, num_blocks)
    group_cols = damping.shape[0]
    num_groups = lax.axis_size("cols")
    band = place_band(skew_blocks(grams), block_base, group_cols, num_groups)
    band_whole = butterfly_sum(halve_over(band, "cols"), "rows")
    group_knots = group_cols // KDOF
    yt = band_whole.reshape(group_knots, WIN_KNOTS, KDOF, KDOF).transpose(1, 3, 0, 2)
    yt = yt.reshape(WIN_KNOTS * KDOF, group_cols)
    t = lax.broadcasted_iota(jnp.int32, yt.shape, 0)
    i = lax.broadcasted_iota(jnp.int32, yt.shape, 1)
    yt = yt + jnp.where(t == i % KDOF, damping[None, :], 0.0)
    return band_cholesky(yt, group_cols)


def solution(mesh):
    return jax.shard_map(
        local,
        mesh=mesh,
        in_specs=(
            P(None, None, ("rows", "cols")),
            P(None, None, ("rows", "cols")),
            P(None, ("rows", "cols")),
            P(None, ("rows", "cols")),
            P(("rows", "cols")),
            P(("rows", "cols")),
            P("cols"),
        ),
        out_specs=P("cols", None),
        check_vma=False,
    )
```

```python
import jax
import jax.numpy as jnp
from jax import lax
from jax.sharding import PartitionSpec as P
from jax.experimental import pallas as pl
from jax.experimental.pallas import tpu as pltpu
import functools

KDOF = 6
WIN_KNOTS = 8
PANEL = 8
WIDTH = 256


def gram_kernel(land_ref, pose_ref, seg_ref, frac_ref, len_ref, out_ref):
    num_obs, lanes = seg_ref.shape
    rows = 2 * num_obs
    u = frac_ref[...]
    u_square = u * u
    u_cubed = u_square * u
    basis = (
        (1.0 - u) ** 3 / 6.0,
        (3.0 * u_cubed - 6.0 * u_square + 4.0) / 6.0,
        (-3.0 * u_cubed + 3.0 * u_square + 3.0 * u + 1.0) / 6.0,
        u_cubed / 6.0,
    )
    seg = seg_ref[...]
    obs = lax.broadcasted_iota(jnp.int32, (num_obs, lanes), 0)
    observed = (obs < len_ref[...]).astype(jnp.float32)
    knot = lax.broadcasted_iota(jnp.int32, (WIN_KNOTS, lanes), 0)
    land = []
    knots = []
    for j in range(num_obs):
        seg_j = seg[j:j + 1, :]
        weight = jnp.zeros((WIN_KNOTS, lanes), jnp.float32)
        for k in range(4):
            weight = weight + basis[k][j:j + 1, :] * (seg_j + k == knot).astype(jnp.float32)
        mask = observed[j:j + 1, :]
        for i in range(2):
            r = 2 * j + i
            land.append(land_ref[r] * mask)
            pose = pose_ref[r] * mask
            knots.append(jnp.concatenate([pose[e:e + 1, :] * weight for e in range(KDOF)], axis=0))
    for k in range(3):
        column = [land[r][k:k + 1, :] for r in range(k, rows)]
        total = column[0] * column[0]
        for x in column[1:]:
            total = total + x * x
        length = jnp.sqrt(total)
        signum = jnp.where(column[0] >= 0.0, 1.0, -1.0)
        vector = [column[0] + signum * length] + column[1:]
        vv = vector[0] * vector[0]
        for x in vector[1:]:
            vv = vv + x * x
        scale = 2.0 / vv
        for mats in (land, knots):
            proj = vector[0] * mats[k]
            for idx in range(1, rows - k):
                proj = proj + vector[idx] * mats[k + idx]
            for idx in range(rows - k):
                mats[k + idx] = mats[k + idx] - (scale * vector[idx]) * proj
    reduced = jnp.concatenate(knots[3:], axis=1)
    out_ref[0] = lax.dot_general(reduced, reduced, (((1,), (1,)), ((), ())),
                                 precision=lax.Precision.HIGHEST, preferred_element_type=jnp.float32)


def block_grams_kernel(land_jac, pose_jac, segment, knot_frac, track_len, num_blocks):
    rows, ldim, landmarks = land_jac.shape
    pdim = pose_jac.shape[1]
    num_obs = segment.shape[0]
    blk = landmarks // num_blocks
    width = WIN_KNOTS * KDOF
    return pl.pallas_call(
        gram_kernel,
        out_shape=jax.ShapeDtypeStruct((num_blocks, width, width), jnp.float32),
        grid=(num_blocks,),
        in_specs=[
            pl.BlockSpec((rows, ldim, blk), lambda b: (0, 0, b)),
            pl.BlockSpec((rows, pdim, blk), lambda b: (0, 0, b)),
            pl.BlockSpec((num_obs, blk), lambda b: (0, b)),
            pl.BlockSpec((num_obs, blk), lambda b: (0, b)),
            pl.BlockSpec((1, blk), lambda b: (0, b)),
        ],
        out_specs=pl.BlockSpec((1, width, width), lambda b: (b, 0, 0)),
    )(land_jac, pose_jac, segment, knot_frac, track_len.reshape(1, landmarks))


def skew_blocks(grams):
    num_blocks = grams.shape[0]
    g5 = grams.reshape(num_blocks, KDOF, WIN_KNOTS, KDOF, WIN_KNOTS).transpose(0, 2, 1, 4, 3)
    k1 = lax.broadcasted_iota(jnp.int32, (WIN_KNOTS, WIN_KNOTS, WIN_KNOTS), 0)
    k2 = lax.broadcasted_iota(jnp.int32, (WIN_KNOTS, WIN_KNOTS, WIN_KNOTS), 1)
    d = lax.broadcasted_iota(jnp.int32, (WIN_KNOTS, WIN_KNOTS, WIN_KNOTS), 2)
    pick = (k2 == k1 + d).astype(jnp.float32)
    return jnp.einsum("bienf,ind->bidef", g5, pick, precision=lax.Precision.HIGHEST)


def place_band(skewed, block_start, group_cols, num_groups):
    num_blocks = skewed.shape[0]
    group_knots = group_cols // KDOF
    rows = num_groups * group_knots
    target = (block_start // group_knots) * group_knots + block_start % group_knots
    target = target[:, None] + jnp.arange(WIN_KNOTS, dtype=jnp.int32)[None, :]
    row_id = lax.broadcasted_iota(jnp.int32, (rows, num_blocks, WIN_KNOTS), 0)
    onehot = (row_id == target[None]).astype(jnp.float32).reshape(rows, num_blocks * WIN_KNOTS)
    flat = skewed.reshape(num_blocks * WIN_KNOTS, WIN_KNOTS * KDOF * KDOF)
    return jnp.dot(onehot, flat, precision=lax.Precision.HIGHEST)


def band_chol_kernel(n, band_w, yt_ref, out_ref, w_ref, r_ref):
    w_ref[...] = jnp.zeros_like(w_ref)
    r_ref[...] = jnp.zeros_like(r_ref)
    lanes = lax.broadcasted_iota(jnp.int32, (band_w, WIDTH), 1)
    for k in range(n // KDOF):
        lo = KDOF * k
        tile = (lo // 128) * 128
        blk = yt_ref[:, tile:tile + WIDTH]
        keep = (lanes >= lo - tile) & (lanes < lo - tile + KDOF)
        w_ref[lo:lo + band_w, tile:tile + WIDTH] += jnp.where(keep, blk, 0.0)
    tiles = n // 128
    ri = lax.broadcasted_iota(jnp.int32, (128, 128), 0)
    ci = lax.broadcasted_iota(jnp.int32, (128, 128), 1)
    for a in range(tiles):
        for b in (a, a + 1):
            if b >= tiles:
                continue
            low = w_ref[128 * a:128 * a + 128, 128 * b:128 * b + 128]
            mirror = w_ref[128 * b:128 * b + 128, 128 * a:128 * a + 128].T
            upper = (ci + 128 * b) // KDOF > (ri + 128 * a) // KDOF
            w_ref[128 * a:128 * a + 128, 128 * b:128 * b + 128] = jnp.where(upper, mirror, low)

    rows = PANEL + band_w
    lane = lax.broadcasted_iota(jnp.int32, (rows, WIDTH), 1)
    row = lax.broadcasted_iota(jnp.int32, (rows, 1), 0)

    def panel(p, carry):
        j0 = pl.multiple_of(p * PANEL, PANEL)
        base = pl.multiple_of((p // (128 // PANEL)) * 128, 128)
        off = j0 - base
        blk = w_ref[pl.ds(j0, rows), pl.ds(base, WIDTH)]
        first = blk[:, :128]
        lane_first = lane[:, :128]
        cols = [jnp.sum(jnp.where(lane_first == off + t, first, 0.0), axis=1, keepdims=True)
                for t in range(PANEL)]
        lcols = []
        invs = []
        for t in range(PANEL):
            inv = lax.rsqrt(cols[t][t:t + 1, :])
            lcol = jnp.where(row >= t, cols[t] * inv, 0.0)
            lcols.append(lcol)
            invs.append(inv)
            for t2 in range(t + 1, PANEL):
                cols[t2] = cols[t2] - lcol * lcol[t2:t2 + 1, :]
        rrows = []
        for t in range(PANEL):
            acc = blk[t:t + 1, :]
            for t1 in range(t):
                acc = acc - lcols[t1][t:t + 1, :] * rrows[t1]
            rrows.append(jnp.where(lane[0:1, :] >= off + t, acc * invs[t], 0.0))
        r_ref[pl.ds(j0, PANEL), pl.ds(base, WIDTH)] = jnp.concatenate(rrows, axis=0)
        trail = blk[PANEL:, :]
        for t in range(PANEL):
            trail = trail - lcols[t][PANEL:, :] * rrows[t]
        start = pl.multiple_of(j0 + PANEL, PANEL)
        w_ref[pl.ds(start, band_w), pl.ds(base, WIDTH)] = trail
        return carry

    lax.fori_loop(0, n // PANEL, panel, 0)
    out_ref[...] = r_ref[0:n, 0:n]


def band_cholesky(yt, n):
    band_w = yt.shape[0]
    padded = n + 128
    yt = jnp.pad(yt, ((0, 0), (0, padded - n)))
    return pl.pallas_call(
        functools.partial(band_chol_kernel, n, band_w),
        out_shape=jax.ShapeDtypeStruct((n, n), jnp.float32),
        in_specs=[pl.BlockSpec(memory_space=pltpu.VMEM)],
        out_specs=pl.BlockSpec(memory_space=pltpu.VMEM),
        scratch_shapes=[
            pltpu.VMEM((n + 64, padded), jnp.float32),
            pltpu.VMEM((n, padded), jnp.float32),
        ],
    )(yt)


def halve_over(band, axis):
    n = lax.axis_size(axis)
    c = lax.axis_index(axis)
    size = band.shape[0]
    s = n // 2
    while s >= 1:
        half = size // 2
        bit = (c // s) % 2
        keep = lax.dynamic_slice_in_dim(band, bit * half, half, 0)
        send = lax.dynamic_slice_in_dim(band, (1 - bit) * half, half, 0)
        band = keep + lax.ppermute(send, axis, [(i, i ^ s) for i in range(n)])
        size = half
        s //= 2
    return band


def butterfly_sum(band, axis):
    n = lax.axis_size(axis)
    s = 1
    while s < n:
        band = band + lax.ppermute(band, axis, [(i, i ^ s) for i in range(n)])
        s *= 2
    return band


def local(land_jac, pose_jac, segment, knot_frac, track_len, block_base, damping):
    num_blocks = block_base.shape[0]
    grams = block_grams_kernel(land_jac, pose_jac, segment, knot_frac, track_len, num_blocks)
    group_cols = damping.shape[0]
    num_groups = lax.axis_size("cols")
    band = place_band(skew_blocks(grams), block_base, group_cols, num_groups)
    band_whole = butterfly_sum(halve_over(band, "cols"), "rows")
    group_knots = group_cols // KDOF
    yt = band_whole.reshape(group_knots, WIN_KNOTS, KDOF, KDOF).transpose(1, 3, 0, 2)
    yt = yt.reshape(WIN_KNOTS * KDOF, group_cols)
    t = lax.broadcasted_iota(jnp.int32, yt.shape, 0)
    i = lax.broadcasted_iota(jnp.int32, yt.shape, 1)
    yt = yt + jnp.where(t == i % KDOF, damping[None, :], 0.0)
    return band_cholesky(yt, group_cols)


def solution(mesh):
    return jax.shard_map(
        local,
        mesh=mesh,
        in_specs=(
            P(None, None, ("rows", "cols")),
            P(None, None, ("rows", "cols")),
            P(None, ("rows", "cols")),
            P(None, ("rows", "cols")),
            P(("rows", "cols")),
            P(("rows", "cols")),
            P("cols"),
        ),
        out_specs=P("cols", None),
        check_vma=False,
    )
```

```python
import jax
import jax.numpy as jnp
from jax import lax
from jax.sharding import PartitionSpec as P
from jax.experimental import pallas as pl
from jax.experimental.pallas import tpu as pltpu
import functools

KDOF = 6
WIN_KNOTS = 8
PANEL = 8
WIDTH = 256


def gram_kernel(land_ref, pose_ref, seg_ref, frac_ref, len_ref, out_ref):
    num_obs, lanes = seg_ref.shape
    rows = 2 * num_obs
    u = frac_ref[...]
    u_square = u * u
    u_cubed = u_square * u
    basis = (
        (1.0 - u) ** 3 / 6.0,
        (3.0 * u_cubed - 6.0 * u_square + 4.0) / 6.0,
        (-3.0 * u_cubed + 3.0 * u_square + 3.0 * u + 1.0) / 6.0,
        u_cubed / 6.0,
    )
    seg = seg_ref[...]
    obs = lax.broadcasted_iota(jnp.int32, (num_obs, lanes), 0)
    observed = (obs < len_ref[...]).astype(jnp.float32)
    knot = lax.broadcasted_iota(jnp.int32, (WIN_KNOTS, lanes), 0)
    land = []
    knots = []
    for j in range(num_obs):
        seg_j = seg[j:j + 1, :]
        weight = jnp.zeros((WIN_KNOTS, lanes), jnp.float32)
        for k in range(4):
            weight = weight + basis[k][j:j + 1, :] * (seg_j + k == knot).astype(jnp.float32)
        mask = observed[j:j + 1, :]
        for i in range(2):
            r = 2 * j + i
            land.append(land_ref[r] * mask)
            pose = pose_ref[r] * mask
            knots.append(jnp.concatenate([pose[e:e + 1, :] * weight for e in range(KDOF)], axis=0))
    for k in range(3):
        column = [land[r][k:k + 1, :] for r in range(k, rows)]
        total = column[0] * column[0]
        for x in column[1:]:
            total = total + x * x
        length = jnp.sqrt(total)
        signum = jnp.where(column[0] >= 0.0, 1.0, -1.0)
        vector = [column[0] + signum * length] + column[1:]
        vv = vector[0] * vector[0]
        for x in vector[1:]:
            vv = vv + x * x
        scale = 2.0 / vv
        for mats in (land, knots):
            proj = vector[0] * mats[k]
            for idx in range(1, rows - k):
                proj = proj + vector[idx] * mats[k + idx]
            for idx in range(rows - k):
                mats[k + idx] = mats[k + idx] - (scale * vector[idx]) * proj
    for s in range(out_ref.shape[0]):
        reduced = jnp.concatenate([m[:, 128 * s:128 * (s + 1)] for m in knots[3:]], axis=1)
        out_ref[s] = lax.dot_general(reduced, reduced, (((1,), (1,)), ((), ())),
                                     precision=lax.Precision.HIGHEST, preferred_element_type=jnp.float32)


def block_grams_kernel(land_jac, pose_jac, segment, knot_frac, track_len, num_blocks, per_step=1):
    rows, ldim, landmarks = land_jac.shape
    pdim = pose_jac.shape[1]
    num_obs = segment.shape[0]
    sub = landmarks // num_blocks
    blk = sub * per_step
    width = WIN_KNOTS * KDOF
    return pl.pallas_call(
        gram_kernel,
        out_shape=jax.ShapeDtypeStruct((num_blocks, width, width), jnp.float32),
        grid=(num_blocks // per_step,),
        in_specs=[
            pl.BlockSpec((rows, ldim, blk), lambda b: (0, 0, b)),
            pl.BlockSpec((rows, pdim, blk), lambda b: (0, 0, b)),
            pl.BlockSpec((num_obs, blk), lambda b: (0, b)),
            pl.BlockSpec((num_obs, blk), lambda b: (0, b)),
            pl.BlockSpec((1, blk), lambda b: (0, b)),
        ],
        out_specs=pl.BlockSpec((per_step, width, width), lambda b: (b, 0, 0)),
    )(land_jac, pose_jac, segment, knot_frac, track_len.reshape(1, landmarks))


def skew_blocks(grams):
    num_blocks = grams.shape[0]
    g5 = grams.reshape(num_blocks, KDOF, WIN_KNOTS, KDOF, WIN_KNOTS).transpose(0, 2, 1, 4, 3)
    k1 = lax.broadcasted_iota(jnp.int32, (WIN_KNOTS, WIN_KNOTS, WIN_KNOTS), 0)
    k2 = lax.broadcasted_iota(jnp.int32, (WIN_KNOTS, WIN_KNOTS, WIN_KNOTS), 1)
    d = lax.broadcasted_iota(jnp.int32, (WIN_KNOTS, WIN_KNOTS, WIN_KNOTS), 2)
    pick = (k2 == k1 + d).astype(jnp.float32)
    return jnp.einsum("bienf,ind->bidef", g5, pick, precision=lax.Precision.HIGHEST)


def place_band(skewed, block_start, group_cols, num_groups):
    num_blocks = skewed.shape[0]
    group_knots = group_cols // KDOF
    rows = num_groups * group_knots
    target = (block_start // group_knots) * group_knots + block_start % group_knots
    target = target[:, None] + jnp.arange(WIN_KNOTS, dtype=jnp.int32)[None, :]
    row_id = lax.broadcasted_iota(jnp.int32, (rows, num_blocks, WIN_KNOTS), 0)
    onehot = (row_id == target[None]).astype(jnp.float32).reshape(rows, num_blocks * WIN_KNOTS)
    flat = skewed.reshape(num_blocks * WIN_KNOTS, WIN_KNOTS * KDOF * KDOF)
    return jnp.dot(onehot, flat, precision=lax.Precision.HIGHEST)


def band_chol_kernel(n, band_w, yt_ref, out_ref, w_ref, r_ref):
    w_ref[...] = jnp.zeros_like(w_ref)
    r_ref[...] = jnp.zeros_like(r_ref)
    lanes = lax.broadcasted_iota(jnp.int32, (band_w, WIDTH), 1)
    for k in range(n // KDOF):
        lo = KDOF * k
        tile = (lo // 128) * 128
        blk = yt_ref[:, tile:tile + WIDTH]
        keep = (lanes >= lo - tile) & (lanes < lo - tile + KDOF)
        w_ref[lo:lo + band_w, tile:tile + WIDTH] += jnp.where(keep, blk, 0.0)
    tiles = n // 128
    ri = lax.broadcasted_iota(jnp.int32, (128, 128), 0)
    ci = lax.broadcasted_iota(jnp.int32, (128, 128), 1)
    for a in range(tiles):
        for b in (a, a + 1):
            if b >= tiles:
                continue
            low = w_ref[128 * a:128 * a + 128, 128 * b:128 * b + 128]
            mirror = w_ref[128 * b:128 * b + 128, 128 * a:128 * a + 128].T
            upper = (ci + 128 * b) // KDOF > (ri + 128 * a) // KDOF
            w_ref[128 * a:128 * a + 128, 128 * b:128 * b + 128] = jnp.where(upper, mirror, low)

    rows = PANEL + band_w
    lane = lax.broadcasted_iota(jnp.int32, (rows, WIDTH), 1)
    row = lax.broadcasted_iota(jnp.int32, (rows, 1), 0)

    def panel(p, carry):
        j0 = pl.multiple_of(p * PANEL, PANEL)
        base = pl.multiple_of((p // (128 // PANEL)) * 128, 128)
        off = j0 - base
        blk = w_ref[pl.ds(j0, rows), pl.ds(base, WIDTH)]
        first = blk[:, :128]
        lane_first = lane[:, :128]
        cols = [jnp.sum(jnp.where(lane_first == off + t, first, 0.0), axis=1, keepdims=True)
                for t in range(PANEL)]
        lcols = []
        invs = []
        for t in range(PANEL):
            inv = lax.rsqrt(cols[t][t:t + 1, :])
            lcol = jnp.where(row >= t, cols[t] * inv, 0.0)
            lcols.append(lcol)
            invs.append(inv)
            for t2 in range(t + 1, PANEL):
                cols[t2] = cols[t2] - lcol * lcol[t2:t2 + 1, :]
        rrows = []
        for t in range(PANEL):
            acc = blk[t:t + 1, :]
            for t1 in range(t):
                acc = acc - lcols[t1][t:t + 1, :] * rrows[t1]
            rrows.append(jnp.where(lane[0:1, :] >= off + t, acc * invs[t], 0.0))
        r_ref[pl.ds(j0, PANEL), pl.ds(base, WIDTH)] = jnp.concatenate(rrows, axis=0)
        trail = blk[PANEL:, :]
        for t in range(PANEL):
            trail = trail - lcols[t][PANEL:, :] * rrows[t]
        start = pl.multiple_of(j0 + PANEL, PANEL)
        w_ref[pl.ds(start, band_w), pl.ds(base, WIDTH)] = trail
        return carry

    lax.fori_loop(0, n // PANEL, panel, 0)
    out_ref[...] = r_ref[0:n, 0:n]


def band_cholesky(yt, n):
    band_w = yt.shape[0]
    padded = n + 128
    yt = jnp.pad(yt, ((0, 0), (0, padded - n)))
    return pl.pallas_call(
        functools.partial(band_chol_kernel, n, band_w),
        out_shape=jax.ShapeDtypeStruct((n, n), jnp.float32),
        in_specs=[pl.BlockSpec(memory_space=pltpu.VMEM)],
        out_specs=pl.BlockSpec(memory_space=pltpu.VMEM),
        scratch_shapes=[
            pltpu.VMEM((n + 64, padded), jnp.float32),
            pltpu.VMEM((n, padded), jnp.float32),
        ],
    )(yt)


def halve_over(band, axis):
    n = lax.axis_size(axis)
    c = lax.axis_index(axis)
    size = band.shape[0]
    s = n // 2
    while s >= 1:
        half = size // 2
        bit = (c // s) % 2
        keep = lax.dynamic_slice_in_dim(band, bit * half, half, 0)
        send = lax.dynamic_slice_in_dim(band, (1 - bit) * half, half, 0)
        band = keep + lax.ppermute(send, axis, [(i, i ^ s) for i in range(n)])
        size = half
        s //= 2
    return band


def butterfly_sum(band, axis):
    n = lax.axis_size(axis)
    s = 1
    while s < n:
        band = band + lax.ppermute(band, axis, [(i, i ^ s) for i in range(n)])
        s *= 2
    return band


def local(land_jac, pose_jac, segment, knot_frac, track_len, block_base, damping):
    num_blocks = block_base.shape[0]
    grams = block_grams_kernel(land_jac, pose_jac, segment, knot_frac, track_len, num_blocks, 4)
    group_cols = damping.shape[0]
    num_groups = lax.axis_size("cols")
    band = place_band(skew_blocks(grams), block_base, group_cols, num_groups)
    band_whole = butterfly_sum(halve_over(band, "cols"), "rows")
    group_knots = group_cols // KDOF
    yt = band_whole.reshape(group_knots, WIN_KNOTS, KDOF, KDOF).transpose(1, 3, 0, 2)
    yt = yt.reshape(WIN_KNOTS * KDOF, group_cols)
    t = lax.broadcasted_iota(jnp.int32, yt.shape, 0)
    i = lax.broadcasted_iota(jnp.int32, yt.shape, 1)
    yt = yt + jnp.where(t == i % KDOF, damping[None, :], 0.0)
    return band_cholesky(yt, group_cols)


def solution(mesh):
    return jax.shard_map(
        local,
        mesh=mesh,
        in_specs=(
            P(None, None, ("rows", "cols")),
            P(None, None, ("rows", "cols")),
            P(None, ("rows", "cols")),
            P(None, ("rows", "cols")),
            P(("rows", "cols")),
            P(("rows", "cols")),
            P("cols"),
        ),
        out_specs=P("cols", None),
        check_vma=False,
    )
```

```python
import jax
import jax.numpy as jnp
from jax import lax
from jax.sharding import PartitionSpec as P
from jax.experimental import pallas as pl
from jax.experimental.pallas import tpu as pltpu
import functools

KDOF = 6
WIN_KNOTS = 8
PANEL = 8
WIDTH = 256


def gram_kernel(land_ref, pose_ref, seg_ref, frac_ref, len_ref, out_ref):
    num_obs, lanes = seg_ref.shape
    rows = 2 * num_obs
    u = frac_ref[...]
    u_square = u * u
    u_cubed = u_square * u
    basis = (
        (1.0 - u) ** 3 / 6.0,
        (3.0 * u_cubed - 6.0 * u_square + 4.0) / 6.0,
        (-3.0 * u_cubed + 3.0 * u_square + 3.0 * u + 1.0) / 6.0,
        u_cubed / 6.0,
    )
    seg = seg_ref[...]
    obs = lax.broadcasted_iota(jnp.int32, (num_obs, lanes), 0)
    observed = (obs < len_ref[...]).astype(jnp.float32)
    knot = lax.broadcasted_iota(jnp.int32, (WIN_KNOTS, lanes), 0)
    land = []
    knots = []
    for j in range(num_obs):
        seg_j = seg[j:j + 1, :]
        weight = jnp.zeros((WIN_KNOTS, lanes), jnp.float32)
        for k in range(4):
            weight = weight + basis[k][j:j + 1, :] * (seg_j + k == knot).astype(jnp.float32)
        mask = observed[j:j + 1, :]
        for i in range(2):
            r = 2 * j + i
            land.append(land_ref[r] * mask)
            pose = pose_ref[r] * mask
            knots.append(jnp.concatenate([pose[e:e + 1, :] * weight for e in range(KDOF)], axis=0))
    for k in range(3):
        column = [land[r][k:k + 1, :] for r in range(k, rows)]
        total = column[0] * column[0]
        for x in column[1:]:
            total = total + x * x
        length = jnp.sqrt(total)
        signum = jnp.where(column[0] >= 0.0, 1.0, -1.0)
        vector = [column[0] + signum * length] + column[1:]
        vv = vector[0] * vector[0]
        for x in vector[1:]:
            vv = vv + x * x
        scale = 2.0 / vv
        for mats in (land, knots):
            proj = vector[0] * mats[k]
            for idx in range(1, rows - k):
                proj = proj + vector[idx] * mats[k + idx]
            for idx in range(rows - k):
                mats[k + idx] = mats[k + idx] - (scale * vector[idx]) * proj
    for s in range(out_ref.shape[0]):
        reduced = jnp.concatenate([m[:, 128 * s:128 * (s + 1)] for m in knots[3:]], axis=1)
        out_ref[s] = lax.dot_general(reduced, reduced, (((1,), (1,)), ((), ())),
                                     precision=lax.Precision.HIGHEST, preferred_element_type=jnp.float32)


def block_grams_kernel(land_jac, pose_jac, segment, knot_frac, track_len, num_blocks, per_step=1):
    rows, ldim, landmarks = land_jac.shape
    pdim = pose_jac.shape[1]
    num_obs = segment.shape[0]
    sub = landmarks // num_blocks
    blk = sub * per_step
    width = WIN_KNOTS * KDOF
    return pl.pallas_call(
        gram_kernel,
        out_shape=jax.ShapeDtypeStruct((num_blocks, width, width), jnp.float32),
        grid=(num_blocks // per_step,),
        in_specs=[
            pl.BlockSpec((rows, ldim, blk), lambda b: (0, 0, b)),
            pl.BlockSpec((rows, pdim, blk), lambda b: (0, 0, b)),
            pl.BlockSpec((num_obs, blk), lambda b: (0, b)),
            pl.BlockSpec((num_obs, blk), lambda b: (0, b)),
            pl.BlockSpec((1, blk), lambda b: (0, b)),
        ],
        out_specs=pl.BlockSpec((per_step, width, width), lambda b: (b, 0, 0)),
    )(land_jac, pose_jac, segment, knot_frac, track_len.reshape(1, landmarks))


def skew_blocks(grams):
    num_blocks = grams.shape[0]
    g5 = grams.reshape(num_blocks, KDOF, WIN_KNOTS, KDOF, WIN_KNOTS).transpose(0, 2, 1, 4, 3)
    k1 = lax.broadcasted_iota(jnp.int32, (WIN_KNOTS, WIN_KNOTS, WIN_KNOTS), 0)
    k2 = lax.broadcasted_iota(jnp.int32, (WIN_KNOTS, WIN_KNOTS, WIN_KNOTS), 1)
    d = lax.broadcasted_iota(jnp.int32, (WIN_KNOTS, WIN_KNOTS, WIN_KNOTS), 2)
    pick = (k2 == k1 + d).astype(jnp.float32)
    return jnp.einsum("bienf,ind->bidef", g5, pick, precision=lax.Precision.HIGHEST)


def place_band(skewed, block_start, group_cols, num_groups):
    num_blocks = skewed.shape[0]
    group_knots = group_cols // KDOF
    rows = num_groups * group_knots
    target = (block_start // group_knots) * group_knots + block_start % group_knots
    target = target[:, None] + jnp.arange(WIN_KNOTS, dtype=jnp.int32)[None, :]
    row_id = lax.broadcasted_iota(jnp.int32, (rows, num_blocks, WIN_KNOTS), 0)
    onehot = (row_id == target[None]).astype(jnp.float32).reshape(rows, num_blocks * WIN_KNOTS)
    flat = skewed.reshape(num_blocks * WIN_KNOTS, WIN_KNOTS * KDOF * KDOF)
    return jnp.dot(onehot, flat, precision=lax.Precision.HIGHEST)


def band_chol_kernel(n, band_w, yt_ref, out_ref, w_ref, r_ref):
    w_ref[...] = jnp.zeros_like(w_ref)
    r_ref[...] = jnp.zeros_like(r_ref)
    lanes = lax.broadcasted_iota(jnp.int32, (band_w, WIDTH), 1)
    for k in range(n // KDOF):
        lo = KDOF * k
        tile = (lo // 128) * 128
        blk = yt_ref[:, tile:tile + WIDTH]
        keep = (lanes >= lo - tile) & (lanes < lo - tile + KDOF)
        w_ref[lo:lo + band_w, tile:tile + WIDTH] += jnp.where(keep, blk, 0.0)
    tiles = n // 128
    ri = lax.broadcasted_iota(jnp.int32, (128, 128), 0)
    ci = lax.broadcasted_iota(jnp.int32, (128, 128), 1)
    for a in range(tiles):
        for b in (a, a + 1):
            if b >= tiles:
                continue
            low = w_ref[128 * a:128 * a + 128, 128 * b:128 * b + 128]
            mirror = w_ref[128 * b:128 * b + 128, 128 * a:128 * a + 128].T
            upper = (ci + 128 * b) // KDOF > (ri + 128 * a) // KDOF
            w_ref[128 * a:128 * a + 128, 128 * b:128 * b + 128] = jnp.where(upper, mirror, low)

    rows = PANEL + band_w
    lane = lax.broadcasted_iota(jnp.int32, (rows, WIDTH), 1)
    row = lax.broadcasted_iota(jnp.int32, (rows, 1), 0)

    def panel(p, blk):
        j0 = pl.multiple_of(p * PANEL, PANEL)
        base = pl.multiple_of((p // (128 // PANEL)) * 128, 128)
        off = j0 - base
        first = blk[:, :128]
        lane_first = lane[:, :128]
        cols = [jnp.sum(jnp.where(lane_first == off + t, first, 0.0), axis=1, keepdims=True)
                for t in range(PANEL)]
        lcols = []
        invs = []
        for t in range(PANEL):
            inv = lax.rsqrt(cols[t][t:t + 1, :])
            lcol = jnp.where(row >= t, cols[t] * inv, 0.0)
            lcols.append(lcol)
            invs.append(inv)
            for t2 in range(t + 1, PANEL):
                cols[t2] = cols[t2] - lcol * lcol[t2:t2 + 1, :]
        rrows = []
        for t in range(PANEL):
            acc = blk[t:t + 1, :]
            for t1 in range(t):
                acc = acc - lcols[t1][t:t + 1, :] * rrows[t1]
            rrows.append(jnp.where(lane[0:1, :] >= off + t, acc * invs[t], 0.0))
        r_ref[pl.ds(j0, PANEL), pl.ds(base, WIDTH)] = jnp.concatenate(rrows, axis=0)
        trail = blk[PANEL:, :]
        for t in range(PANEL):
            trail = trail - lcols[t][PANEL:, :] * rrows[t]
        nxt = jnp.minimum(((p + 1) // (128 // PANEL)) * 128, w_ref.shape[1] - WIDTH)
        nxt = pl.multiple_of(nxt, 128)
        moved = jnp.concatenate([trail[:, 128:], jnp.zeros((band_w, WIDTH - 128), jnp.float32)], axis=1)
        trail = jnp.where(nxt != base, moved, trail)
        fresh = w_ref[pl.ds(pl.multiple_of(j0 + rows, PANEL), PANEL), pl.ds(nxt, WIDTH)]
        return jnp.concatenate([trail, fresh], axis=0)

    lax.fori_loop(0, n // PANEL, panel, w_ref[0:rows, 0:WIDTH])
    out_ref[...] = r_ref[0:n, 0:n]


def band_cholesky(yt, n):
    band_w = yt.shape[0]
    padded = n + 128
    yt = jnp.pad(yt, ((0, 0), (0, padded - n)))
    return pl.pallas_call(
        functools.partial(band_chol_kernel, n, band_w),
        out_shape=jax.ShapeDtypeStruct((n, n), jnp.float32),
        in_specs=[pl.BlockSpec(memory_space=pltpu.VMEM)],
        out_specs=pl.BlockSpec(memory_space=pltpu.VMEM),
        scratch_shapes=[
            pltpu.VMEM((n + 64, padded), jnp.float32),
            pltpu.VMEM((n, padded), jnp.float32),
        ],
    )(yt)


def scatter_sum(band, axis):
    n = lax.axis_size(axis)
    got = lax.all_to_all(band, axis, 0, 0, tiled=True)
    got = got.reshape(n, band.shape[0] // n, band.shape[1])
    total = got[0]
    for j in range(1, n):
        total = total + got[j]
    return total


def butterfly_sum(band, axis):
    n = lax.axis_size(axis)
    s = 1
    while s < n:
        band = band + lax.ppermute(band, axis, [(i, i ^ s) for i in range(n)])
        s *= 2
    return band


def local(land_jac, pose_jac, segment, knot_frac, track_len, block_base, damping):
    num_blocks = block_base.shape[0]
    grams = block_grams_kernel(land_jac, pose_jac, segment, knot_frac, track_len, num_blocks, 4)
    group_cols = damping.shape[0]
    num_groups = lax.axis_size("cols")
    band = place_band(skew_blocks(grams), block_base, group_cols, num_groups)
    band_whole = butterfly_sum(scatter_sum(band, "cols"), "rows")
    group_knots = group_cols // KDOF
    yt = band_whole.reshape(group_knots, WIN_KNOTS, KDOF, KDOF).transpose(1, 3, 0, 2)
    yt = yt.reshape(WIN_KNOTS * KDOF, group_cols)
    t = lax.broadcasted_iota(jnp.int32, yt.shape, 0)
    i = lax.broadcasted_iota(jnp.int32, yt.shape, 1)
    yt = yt + jnp.where(t == i % KDOF, damping[None, :], 0.0)
    return band_cholesky(yt, group_cols)


def solution(mesh):
    return jax.shard_map(
        local,
        mesh=mesh,
        in_specs=(
            P(None, None, ("rows", "cols")),
            P(None, None, ("rows", "cols")),
            P(None, ("rows", "cols")),
            P(None, ("rows", "cols")),
            P(("rows", "cols")),
            P(("rows", "cols")),
            P("cols"),
        ),
        out_specs=P("cols", None),
        check_vma=False,
    )
```

```python
import jax
import jax.numpy as jnp
from jax import lax
from jax.sharding import PartitionSpec as P
from jax.experimental import pallas as pl
from jax.experimental.pallas import tpu as pltpu
import functools

KDOF = 6
WIN_KNOTS = 8
PANEL = 8
WIDTH = 256


def gram_kernel(ldim, pdim, land_ref, pose_ref, seg_ref, frac_ref, len_ref, out_ref):
    num_obs, lanes = seg_ref.shape
    rows = 2 * num_obs
    u = frac_ref[...]
    u_square = u * u
    u_cubed = u_square * u
    basis = (
        (1.0 - u) ** 3 / 6.0,
        (3.0 * u_cubed - 6.0 * u_square + 4.0) / 6.0,
        (-3.0 * u_cubed + 3.0 * u_square + 3.0 * u + 1.0) / 6.0,
        u_cubed / 6.0,
    )
    seg = seg_ref[...]
    obs = lax.broadcasted_iota(jnp.int32, (num_obs, lanes), 0)
    observed = (obs < len_ref[...]).astype(jnp.float32)
    knot = lax.broadcasted_iota(jnp.int32, (WIN_KNOTS, lanes), 0)
    land = []
    knots = []
    for j in range(num_obs):
        seg_j = seg[j:j + 1, :]
        weight = jnp.zeros((WIN_KNOTS, lanes), jnp.float32)
        for k in range(4):
            weight = weight + basis[k][j:j + 1, :] * (seg_j + k == knot).astype(jnp.float32)
        mask = observed[j:j + 1, :]
        for i in range(2):
            r = 2 * j + i
            land.append(jnp.concatenate([land_ref[c, r:r + 1, :] for c in range(ldim)], axis=0) * mask)
            knots.append(jnp.concatenate([(pose_ref[e, r:r + 1, :] * mask) * weight for e in range(KDOF)], axis=0))
    for k in range(3):
        column = [land[r][k:k + 1, :] for r in range(k, rows)]
        total = column[0] * column[0]
        for x in column[1:]:
            total = total + x * x
        length = jnp.sqrt(total)
        signum = jnp.where(column[0] >= 0.0, 1.0, -1.0)
        vector = [column[0] + signum * length] + column[1:]
        vv = vector[0] * vector[0]
        for x in vector[1:]:
            vv = vv + x * x
        scale = 2.0 / vv
        for mats in (land, knots):
            proj = vector[0] * mats[k]
            for idx in range(1, rows - k):
                proj = proj + vector[idx] * mats[k + idx]
            for idx in range(rows - k):
                mats[k + idx] = mats[k + idx] - (scale * vector[idx]) * proj
    for s in range(out_ref.shape[0]):
        reduced = jnp.concatenate([m[:, 128 * s:128 * (s + 1)] for m in knots[3:]], axis=1)
        out_ref[s] = lax.dot_general(reduced, reduced, (((1,), (1,)), ((), ())),
                                     precision=lax.Precision.HIGHEST, preferred_element_type=jnp.float32)


def block_grams_kernel(land_jac, pose_jac, segment, knot_frac, track_len, num_blocks, per_step=1):
    rows, ldim, landmarks = land_jac.shape
    pdim = pose_jac.shape[1]
    num_obs = segment.shape[0]
    sub = landmarks // num_blocks
    blk = sub * per_step
    width = WIN_KNOTS * KDOF
    return pl.pallas_call(
        functools.partial(gram_kernel, ldim, pdim),
        out_shape=jax.ShapeDtypeStruct((num_blocks, width, width), jnp.float32),
        grid=(num_blocks // per_step,),
        in_specs=[
            pl.BlockSpec((ldim, rows, blk), lambda b: (0, 0, b)),
            pl.BlockSpec((pdim, rows, blk), lambda b: (0, 0, b)),
            pl.BlockSpec((num_obs, blk), lambda b: (0, b)),
            pl.BlockSpec((num_obs, blk), lambda b: (0, b)),
            pl.BlockSpec((1, blk), lambda b: (0, b)),
        ],
        out_specs=pl.BlockSpec((per_step, width, width), lambda b: (b, 0, 0)),
    )(jnp.transpose(land_jac, (1, 0, 2)), jnp.transpose(pose_jac, (1, 0, 2)),
      segment, knot_frac, track_len.reshape(1, landmarks))


def skew_blocks(grams):
    num_blocks = grams.shape[0]
    g5 = grams.reshape(num_blocks, KDOF, WIN_KNOTS, KDOF, WIN_KNOTS).transpose(0, 2, 1, 4, 3)
    k1 = lax.broadcasted_iota(jnp.int32, (WIN_KNOTS, WIN_KNOTS, WIN_KNOTS), 0)
    k2 = lax.broadcasted_iota(jnp.int32, (WIN_KNOTS, WIN_KNOTS, WIN_KNOTS), 1)
    d = lax.broadcasted_iota(jnp.int32, (WIN_KNOTS, WIN_KNOTS, WIN_KNOTS), 2)
    pick = (k2 == k1 + d).astype(jnp.float32)
    return jnp.einsum("bienf,ind->bidef", g5, pick, precision=lax.Precision.HIGHEST)


def place_band(skewed, block_start, group_cols, num_groups):
    num_blocks = skewed.shape[0]
    group_knots = group_cols // KDOF
    rows = num_groups * group_knots
    target = (block_start // group_knots) * group_knots + block_start % group_knots
    target = target[:, None] + jnp.arange(WIN_KNOTS, dtype=jnp.int32)[None, :]
    row_id = lax.broadcasted_iota(jnp.int32, (rows, num_blocks, WIN_KNOTS), 0)
    onehot = (row_id == target[None]).astype(jnp.float32).reshape(rows, num_blocks * WIN_KNOTS)
    flat = skewed.reshape(num_blocks * WIN_KNOTS, WIN_KNOTS * KDOF * KDOF)
    return jnp.dot(onehot, flat, precision=lax.Precision.HIGHEST)


def band_chol_kernel(n, band_w, yt_ref, out_ref, w_ref, r_ref):
    w_ref[...] = jnp.zeros_like(w_ref)
    r_ref[...] = jnp.zeros_like(r_ref)
    for k in range(n // KDOF):
        lo = KDOF * k
        tile = (lo // 128) * 128
        span = 128 if lo - tile + KDOF <= 128 else WIDTH
        lanes = lax.broadcasted_iota(jnp.int32, (band_w, span), 1)
        blk = yt_ref[:, tile:tile + span]
        keep = (lanes >= lo - tile) & (lanes < lo - tile + KDOF)
        w_ref[lo:lo + band_w, tile:tile + span] += jnp.where(keep, blk, 0.0)
    tiles = n // 128
    ri = lax.broadcasted_iota(jnp.int32, (128, 128), 0)
    ci = lax.broadcasted_iota(jnp.int32, (128, 128), 1)
    for a in range(tiles):
        for b in (a, a + 1):
            if b >= tiles:
                continue
            low = w_ref[128 * a:128 * a + 128, 128 * b:128 * b + 128]
            mirror = w_ref[128 * b:128 * b + 128, 128 * a:128 * a + 128].T
            upper = (ci + 128 * b) // KDOF > (ri + 128 * a) // KDOF
            w_ref[128 * a:128 * a + 128, 128 * b:128 * b + 128] = jnp.where(upper, mirror, low)

    rows = PANEL + band_w
    lane = lax.broadcasted_iota(jnp.int32, (rows, WIDTH), 1)
    row = lax.broadcasted_iota(jnp.int32, (rows, 1), 0)

    def panel(p, blk):
        j0 = pl.multiple_of(p * PANEL, PANEL)
        base = pl.multiple_of((p // (128 // PANEL)) * 128, 128)
        off = j0 - base
        first = blk[:, :128]
        lane_first = lane[:, :128]
        cols = [jnp.sum(jnp.where(lane_first == off + t, first, 0.0), axis=1, keepdims=True)
                for t in range(PANEL)]
        lcols = []
        invs = []
        for t in range(PANEL):
            inv = lax.rsqrt(cols[t][t:t + 1, :])
            lcol = jnp.where(row >= t, cols[t] * inv, 0.0)
            lcols.append(lcol)
            invs.append(inv)
            for t2 in range(t + 1, PANEL):
                cols[t2] = cols[t2] - lcol * lcol[t2:t2 + 1, :]
        rrows = []
        for t in range(PANEL):
            acc = blk[t:t + 1, :]
            for t1 in range(t):
                acc = acc - lcols[t1][t:t + 1, :] * rrows[t1]
            rrows.append(jnp.where(lane[0:1, :] >= off + t, acc * invs[t], 0.0))
        r_ref[pl.ds(j0, PANEL), pl.ds(base, WIDTH)] = jnp.concatenate(rrows, axis=0)
        trail = blk[PANEL:, :]
        for t in range(PANEL):
            trail = trail - lcols[t][PANEL:, :] * rrows[t]
        nxt = jnp.minimum(((p + 1) // (128 // PANEL)) * 128, w_ref.shape[1] - WIDTH)
        nxt = pl.multiple_of(nxt, 128)
        moved = jnp.concatenate([trail[:, 128:], jnp.zeros((band_w, WIDTH - 128), jnp.float32)], axis=1)
        trail = jnp.where(nxt != base, moved, trail)
        fresh = w_ref[pl.ds(pl.multiple_of(j0 + rows, PANEL), PANEL), pl.ds(nxt, WIDTH)]
        return jnp.concatenate([trail, fresh], axis=0)

    lax.fori_loop(0, n // PANEL, panel, w_ref[0:rows, 0:WIDTH])
    out_ref[...] = r_ref[0:n, 0:n]


def band_cholesky(yt, n):
    band_w = yt.shape[0]
    padded = n + 128
    yt = jnp.pad(yt, ((0, 0), (0, padded - n)))
    return pl.pallas_call(
        functools.partial(band_chol_kernel, n, band_w),
        out_shape=jax.ShapeDtypeStruct((n, n), jnp.float32),
        in_specs=[pl.BlockSpec(memory_space=pltpu.VMEM)],
        out_specs=pl.BlockSpec(memory_space=pltpu.VMEM),
        scratch_shapes=[
            pltpu.VMEM((n + 64, padded), jnp.float32),
            pltpu.VMEM((n, padded), jnp.float32),
        ],
    )(yt)


def scatter_sum(band, axis):
    n = lax.axis_size(axis)
    got = lax.all_to_all(band, axis, 0, 0, tiled=True)
    got = got.reshape(n, band.shape[0] // n, band.shape[1])
    total = got[0]
    for j in range(1, n):
        total = total + got[j]
    return total


def butterfly_sum(band, axis):
    n = lax.axis_size(axis)
    s = 1
    while s < n:
        band = band + lax.ppermute(band, axis, [(i, i ^ s) for i in range(n)])
        s *= 2
    return band


def local(land_jac, pose_jac, segment, knot_frac, track_len, block_base, damping):
    num_blocks = block_base.shape[0]
    grams = block_grams_kernel(land_jac, pose_jac, segment, knot_frac, track_len, num_blocks, 4)
    group_cols = damping.shape[0]
    num_groups = lax.axis_size("cols")
    band = place_band(skew_blocks(grams), block_base, group_cols, num_groups)
    band_whole = butterfly_sum(scatter_sum(band, "cols"), "rows")
    group_knots = group_cols // KDOF
    yt = band_whole.reshape(group_knots, WIN_KNOTS, KDOF, KDOF).transpose(1, 3, 0, 2)
    yt = yt.reshape(WIN_KNOTS * KDOF, group_cols)
    t = lax.broadcasted_iota(jnp.int32, yt.shape, 0)
    i = lax.broadcasted_iota(jnp.int32, yt.shape, 1)
    yt = yt + jnp.where(t == i % KDOF, damping[None, :], 0.0)
    return band_cholesky(yt, group_cols)


def solution(mesh):
    return jax.shard_map(
        local,
        mesh=mesh,
        in_specs=(
            P(None, None, ("rows", "cols")),
            P(None, None, ("rows", "cols")),
            P(None, ("rows", "cols")),
            P(None, ("rows", "cols")),
            P(("rows", "cols")),
            P(("rows", "cols")),
            P("cols"),
        ),
        out_specs=P("cols", None),
        check_vma=False,
    )
```

```python
import jax
import jax.numpy as jnp
from jax import lax
from jax.sharding import PartitionSpec as P
from jax.experimental import pallas as pl
from jax.experimental.pallas import tpu as pltpu
import functools

KDOF = 6
WIN_KNOTS = 8
PANEL = 8
WIDTH = 256


def gram_kernel(ldim, pdim, land_ref, pose_ref, seg_ref, frac_ref, len_ref, out_ref):
    num_obs, lanes = seg_ref.shape
    rows = 2 * num_obs
    u = frac_ref[...]
    u_square = u * u
    u_cubed = u_square * u
    basis = (
        (1.0 - u) ** 3 / 6.0,
        (3.0 * u_cubed - 6.0 * u_square + 4.0) / 6.0,
        (-3.0 * u_cubed + 3.0 * u_square + 3.0 * u + 1.0) / 6.0,
        u_cubed / 6.0,
    )
    seg = seg_ref[...]
    obs = lax.broadcasted_iota(jnp.int32, (num_obs, lanes), 0)
    observed = (obs < len_ref[...]).astype(jnp.float32)
    knot = lax.broadcasted_iota(jnp.int32, (WIN_KNOTS, lanes), 0)
    land = []
    knots = []
    for j in range(num_obs):
        seg_j = seg[j:j + 1, :]
        weight = jnp.zeros((WIN_KNOTS, lanes), jnp.float32)
        for k in range(4):
            weight = weight + basis[k][j:j + 1, :] * (seg_j + k == knot).astype(jnp.float32)
        mask = observed[j:j + 1, :]
        for i in range(2):
            r = 2 * j + i
            land.append(jnp.concatenate([land_ref[c, r:r + 1, :] for c in range(ldim)], axis=0) * mask)
            knots.append(jnp.concatenate([(pose_ref[e, r:r + 1, :] * mask) * weight for e in range(KDOF)], axis=0))
    for k in range(3):
        column = [land[r][k:k + 1, :] for r in range(k, rows)]
        total = column[0] * column[0]
        for x in column[1:]:
            total = total + x * x
        length = jnp.sqrt(total)
        signum = jnp.where(column[0] >= 0.0, 1.0, -1.0)
        vector = [column[0] + signum * length] + column[1:]
        vv = vector[0] * vector[0]
        for x in vector[1:]:
            vv = vv + x * x
        scale = 2.0 / vv
        for mats in (land, knots):
            proj = vector[0] * mats[k]
            for idx in range(1, rows - k):
                proj = proj + vector[idx] * mats[k + idx]
            for idx in range(rows - k):
                mats[k + idx] = mats[k + idx] - (scale * vector[idx]) * proj
    for s in range(out_ref.shape[0]):
        reduced = jnp.concatenate([m[:, 128 * s:128 * (s + 1)] for m in knots[3:]], axis=1)
        out_ref[s] = lax.dot_general(reduced, reduced, (((1,), (1,)), ((), ())),
                                     precision=lax.Precision.HIGHEST, preferred_element_type=jnp.float32)


def block_grams_kernel(land_jac, pose_jac, segment, knot_frac, track_len, num_blocks, per_step=1):
    rows, ldim, landmarks = land_jac.shape
    pdim = pose_jac.shape[1]
    num_obs = segment.shape[0]
    sub = landmarks // num_blocks
    blk = sub * per_step
    width = WIN_KNOTS * KDOF
    return pl.pallas_call(
        functools.partial(gram_kernel, ldim, pdim),
        out_shape=jax.ShapeDtypeStruct((num_blocks, width, width), jnp.float32),
        grid=(num_blocks // per_step,),
        in_specs=[
            pl.BlockSpec((ldim, rows, blk), lambda b: (0, 0, b)),
            pl.BlockSpec((pdim, rows, blk), lambda b: (0, 0, b)),
            pl.BlockSpec((num_obs, blk), lambda b: (0, b)),
            pl.BlockSpec((num_obs, blk), lambda b: (0, b)),
            pl.BlockSpec((1, blk), lambda b: (0, b)),
        ],
        out_specs=pl.BlockSpec((per_step, width, width), lambda b: (b, 0, 0)),
    )(jnp.transpose(land_jac, (1, 0, 2)), jnp.transpose(pose_jac, (1, 0, 2)),
      segment, knot_frac, track_len.reshape(1, landmarks))


def skew_blocks(grams):
    num_blocks = grams.shape[0]
    g5 = grams.reshape(num_blocks, KDOF, WIN_KNOTS, KDOF, WIN_KNOTS).transpose(0, 2, 1, 4, 3)
    k1 = lax.broadcasted_iota(jnp.int32, (WIN_KNOTS, WIN_KNOTS, WIN_KNOTS), 0)
    k2 = lax.broadcasted_iota(jnp.int32, (WIN_KNOTS, WIN_KNOTS, WIN_KNOTS), 1)
    d = lax.broadcasted_iota(jnp.int32, (WIN_KNOTS, WIN_KNOTS, WIN_KNOTS), 2)
    pick = (k2 == k1 + d).astype(jnp.float32)
    return jnp.einsum("bienf,ind->bidef", g5, pick, precision=lax.Precision.HIGHEST)


def place_band(skewed, block_start, group_cols, num_groups):
    num_blocks = skewed.shape[0]
    group_knots = group_cols // KDOF
    rows = num_groups * group_knots
    target = (block_start // group_knots) * group_knots + block_start % group_knots
    target = target[:, None] + jnp.arange(WIN_KNOTS, dtype=jnp.int32)[None, :]
    row_id = lax.broadcasted_iota(jnp.int32, (rows, num_blocks, WIN_KNOTS), 0)
    onehot = (row_id == target[None]).astype(jnp.float32).reshape(rows, num_blocks * WIN_KNOTS)
    flat = skewed.reshape(num_blocks * WIN_KNOTS, WIN_KNOTS * KDOF * KDOF)
    return jnp.dot(onehot, flat, precision=lax.Precision.HIGHEST)


def band_chol_kernel(n, band_w, yt_ref, damp_ref, out_ref, w_ref, r_ref):
    w_ref[...] = jnp.zeros_like(w_ref)
    r_ref[...] = jnp.zeros_like(r_ref)
    for k in range(n // KDOF):
        lo = KDOF * k
        tile = (lo // 128) * 128
        span = 128 if lo - tile + KDOF <= 128 else WIDTH
        lanes = lax.broadcasted_iota(jnp.int32, (band_w, span), 1)
        blk = yt_ref[:, tile:tile + span]
        keep = (lanes >= lo - tile) & (lanes < lo - tile + KDOF)
        w_ref[lo:lo + band_w, tile:tile + span] += jnp.where(keep, blk, 0.0)
    tiles = n // 128
    ri = lax.broadcasted_iota(jnp.int32, (128, 128), 0)
    ci = lax.broadcasted_iota(jnp.int32, (128, 128), 1)
    for a in range(tiles):
        for b in (a, a + 1):
            if b >= tiles:
                continue
            low = w_ref[128 * a:128 * a + 128, 128 * b:128 * b + 128]
            mirror = w_ref[128 * b:128 * b + 128, 128 * a:128 * a + 128].T
            upper = (ci + 128 * b) // KDOF > (ri + 128 * a) // KDOF
            tile_val = jnp.where(upper, mirror, low)
            if a == b:
                tile_val = tile_val + jnp.where(ri == ci, damp_ref[:, 128 * a:128 * a + 128], 0.0)
            w_ref[128 * a:128 * a + 128, 128 * b:128 * b + 128] = tile_val

    rows = PANEL + band_w
    lane = lax.broadcasted_iota(jnp.int32, (rows, WIDTH), 1)
    row = lax.broadcasted_iota(jnp.int32, (rows, 1), 0)

    def panel(p, blk):
        j0 = pl.multiple_of(p * PANEL, PANEL)
        base = pl.multiple_of((p // (128 // PANEL)) * 128, 128)
        off = j0 - base
        first = blk[:, :128]
        lane_first = lane[:, :128]
        cols = [jnp.sum(jnp.where(lane_first == off + t, first, 0.0), axis=1, keepdims=True)
                for t in range(PANEL)]
        lcols = []
        invs = []
        for t in range(PANEL):
            inv = lax.rsqrt(cols[t][t:t + 1, :])
            lcol = jnp.where(row >= t, cols[t] * inv, 0.0)
            lcols.append(lcol)
            invs.append(inv)
            for t2 in range(t + 1, PANEL):
                cols[t2] = cols[t2] - lcol * lcol[t2:t2 + 1, :]
        rrows = []
        for t in range(PANEL):
            acc = blk[t:t + 1, :]
            for t1 in range(t):
                acc = acc - lcols[t1][t:t + 1, :] * rrows[t1]
            rrows.append(jnp.where(lane[0:1, :] >= off + t, acc * invs[t], 0.0))
        r_ref[pl.ds(j0, PANEL), pl.ds(base, WIDTH)] = jnp.concatenate(rrows, axis=0)
        trail = blk[PANEL:, :]
        for t in range(PANEL):
            trail = trail - lcols[t][PANEL:, :] * rrows[t]
        nxt = jnp.minimum(((p + 1) // (128 // PANEL)) * 128, w_ref.shape[1] - WIDTH)
        nxt = pl.multiple_of(nxt, 128)
        moved = jnp.concatenate([trail[:, 128:], jnp.zeros((band_w, WIDTH - 128), jnp.float32)], axis=1)
        trail = jnp.where(nxt != base, moved, trail)
        fresh = w_ref[pl.ds(pl.multiple_of(j0 + rows, PANEL), PANEL), pl.ds(nxt, WIDTH)]
        return jnp.concatenate([trail, fresh], axis=0)

    lax.fori_loop(0, n // PANEL, panel, w_ref[0:rows, 0:WIDTH])
    out_ref[...] = r_ref[0:n, 0:n]


def band_cholesky(yt, damping, n):
    band_w = yt.shape[0]
    padded = n + 128
    return pl.pallas_call(
        functools.partial(band_chol_kernel, n, band_w),
        out_shape=jax.ShapeDtypeStruct((n, n), jnp.float32),
        in_specs=[pl.BlockSpec(memory_space=pltpu.VMEM)] * 2,
        out_specs=pl.BlockSpec(memory_space=pltpu.VMEM),
        scratch_shapes=[
            pltpu.VMEM((n + 64, padded), jnp.float32),
            pltpu.VMEM((n, padded), jnp.float32),
        ],
    )(yt, damping.reshape(1, n))


def scatter_sum(band, axis):
    n = lax.axis_size(axis)
    got = lax.all_to_all(band, axis, 0, 0, tiled=True)
    got = got.reshape(n, band.shape[0] // n, band.shape[1])
    total = got[0]
    for j in range(1, n):
        total = total + got[j]
    return total


def butterfly_sum(band, axis):
    n = lax.axis_size(axis)
    s = 1
    while s < n:
        band = band + lax.ppermute(band, axis, [(i, i ^ s) for i in range(n)])
        s *= 2
    return band


def local(land_jac, pose_jac, segment, knot_frac, track_len, block_base, damping):
    num_blocks = block_base.shape[0]
    grams = block_grams_kernel(land_jac, pose_jac, segment, knot_frac, track_len, num_blocks, 8)
    group_cols = damping.shape[0]
    num_groups = lax.axis_size("cols")
    band = place_band(skew_blocks(grams), block_base, group_cols, num_groups)
    band_whole = butterfly_sum(scatter_sum(band, "cols"), "rows")
    group_knots = group_cols // KDOF
    yt = band_whole.reshape(group_knots, WIN_KNOTS, KDOF, KDOF).transpose(1, 3, 0, 2)
    yt = yt.reshape(WIN_KNOTS * KDOF, group_cols)
    return band_cholesky(yt, damping, group_cols)


def solution(mesh):
    return jax.shard_map(
        local,
        mesh=mesh,
        in_specs=(
            P(None, None, ("rows", "cols")),
            P(None, None, ("rows", "cols")),
            P(None, ("rows", "cols")),
            P(None, ("rows", "cols")),
            P(("rows", "cols")),
            P(("rows", "cols")),
            P("cols"),
        ),
        out_specs=P("cols", None),
        check_vma=False,
    )
```

```python
import jax
import jax.numpy as jnp
from jax import lax
from jax.sharding import PartitionSpec as P
from jax.experimental import pallas as pl
from jax.experimental.pallas import tpu as pltpu
import functools

KDOF = 6
WIN_KNOTS = 8
PANEL = 8
WIDTH = 256


def gram_kernel(ldim, pdim, land_ref, pose_ref, seg_ref, frac_ref, len_ref, out_ref):
    num_obs, lanes = seg_ref.shape
    rows = 2 * num_obs
    u = frac_ref[...]
    u_square = u * u
    u_cubed = u_square * u
    basis = (
        (1.0 - u) ** 3 / 6.0,
        (3.0 * u_cubed - 6.0 * u_square + 4.0) / 6.0,
        (-3.0 * u_cubed + 3.0 * u_square + 3.0 * u + 1.0) / 6.0,
        u_cubed / 6.0,
    )
    seg = seg_ref[...]
    obs = lax.broadcasted_iota(jnp.int32, (num_obs, lanes), 0)
    observed = (obs < len_ref[...]).astype(jnp.float32)
    knot = lax.broadcasted_iota(jnp.int32, (WIN_KNOTS, lanes), 0)
    land = []
    knots = []
    for j in range(num_obs):
        seg_j = seg[j:j + 1, :]
        weight = jnp.zeros((WIN_KNOTS, lanes), jnp.float32)
        for k in range(4):
            weight = weight + basis[k][j:j + 1, :] * (seg_j + k == knot).astype(jnp.float32)
        mask = observed[j:j + 1, :]
        for i in range(2):
            r = 2 * j + i
            land.append(jnp.concatenate([land_ref[c, r:r + 1, :] for c in range(ldim)], axis=0) * mask)
            knots.append(jnp.concatenate([(pose_ref[e, r:r + 1, :] * mask) * weight for e in range(KDOF)], axis=0))
    for k in range(3):
        column = [land[r][k:k + 1, :] for r in range(k, rows)]
        total = column[0] * column[0]
        for x in column[1:]:
            total = total + x * x
        length = jnp.sqrt(total)
        signum = jnp.where(column[0] >= 0.0, 1.0, -1.0)
        vector = [column[0] + signum * length] + column[1:]
        vv = vector[0] * vector[0]
        for x in vector[1:]:
            vv = vv + x * x
        scale = 2.0 / vv
        for mats in (land, knots):
            proj = vector[0] * mats[k]
            for idx in range(1, rows - k):
                proj = proj + vector[idx] * mats[k + idx]
            for idx in range(rows - k):
                mats[k + idx] = mats[k + idx] - (scale * vector[idx]) * proj
    for s in range(out_ref.shape[0]):
        reduced = jnp.concatenate([m[:, 128 * s:128 * (s + 1)] for m in knots[3:]], axis=1)
        out_ref[s] = lax.dot_general(reduced, reduced, (((1,), (1,)), ((), ())),
                                     precision=lax.Precision.HIGH, preferred_element_type=jnp.float32)


def block_grams_kernel(land_jac, pose_jac, segment, knot_frac, track_len, num_blocks, per_step=1):
    rows, ldim, landmarks = land_jac.shape
    pdim = pose_jac.shape[1]
    num_obs = segment.shape[0]
    sub = landmarks // num_blocks
    blk = sub * per_step
    width = WIN_KNOTS * KDOF
    return pl.pallas_call(
        functools.partial(gram_kernel, ldim, pdim),
        out_shape=jax.ShapeDtypeStruct((num_blocks, width, width), jnp.float32),
        grid=(num_blocks // per_step,),
        in_specs=[
            pl.BlockSpec((ldim, rows, blk), lambda b: (0, 0, b)),
            pl.BlockSpec((pdim, rows, blk), lambda b: (0, 0, b)),
            pl.BlockSpec((num_obs, blk), lambda b: (0, b)),
            pl.BlockSpec((num_obs, blk), lambda b: (0, b)),
            pl.BlockSpec((1, blk), lambda b: (0, b)),
        ],
        out_specs=pl.BlockSpec((per_step, width, width), lambda b: (b, 0, 0)),
    )(jnp.transpose(land_jac, (1, 0, 2)), jnp.transpose(pose_jac, (1, 0, 2)),
      segment, knot_frac, track_len.reshape(1, landmarks))


def skew_blocks(grams):
    num_blocks = grams.shape[0]
    g5 = grams.reshape(num_blocks, KDOF, WIN_KNOTS, KDOF, WIN_KNOTS).transpose(0, 2, 1, 4, 3)
    k1 = lax.broadcasted_iota(jnp.int32, (WIN_KNOTS, WIN_KNOTS, WIN_KNOTS), 0)
    k2 = lax.broadcasted_iota(jnp.int32, (WIN_KNOTS, WIN_KNOTS, WIN_KNOTS), 1)
    d = lax.broadcasted_iota(jnp.int32, (WIN_KNOTS, WIN_KNOTS, WIN_KNOTS), 2)
    pick = (k2 == k1 + d).astype(jnp.float32)
    return jnp.einsum("bienf,ind->bidef", g5, pick, precision=lax.Precision.HIGHEST)


def place_band(skewed, block_start, group_cols, num_groups):
    num_blocks = skewed.shape[0]
    group_knots = group_cols // KDOF
    rows = num_groups * group_knots
    target = (block_start // group_knots) * group_knots + block_start % group_knots
    target = target[:, None] + jnp.arange(WIN_KNOTS, dtype=jnp.int32)[None, :]
    row_id = lax.broadcasted_iota(jnp.int32, (rows, num_blocks, WIN_KNOTS), 0)
    onehot = (row_id == target[None]).astype(jnp.float32).reshape(rows, num_blocks * WIN_KNOTS)
    flat = skewed.reshape(num_blocks * WIN_KNOTS, WIN_KNOTS * KDOF * KDOF)
    return jnp.dot(onehot, flat, precision=lax.Precision.HIGHEST)


def band_chol_kernel(n, band_w, yt_ref, damp_ref, out_ref, w_ref, r_ref):
    w_ref[...] = jnp.zeros_like(w_ref)
    r_ref[...] = jnp.zeros_like(r_ref)
    for k in range(n // KDOF):
        lo = KDOF * k
        tile = (lo // 128) * 128
        span = 128 if lo - tile + KDOF <= 128 else WIDTH
        lanes = lax.broadcasted_iota(jnp.int32, (band_w, span), 1)
        blk = yt_ref[:, tile:tile + span]
        keep = (lanes >= lo - tile) & (lanes < lo - tile + KDOF)
        w_ref[lo:lo + band_w, tile:tile + span] += jnp.where(keep, blk, 0.0)
    tiles = n // 128
    ri = lax.broadcasted_iota(jnp.int32, (128, 128), 0)
    ci = lax.broadcasted_iota(jnp.int32, (128, 128), 1)
    for a in range(tiles):
        for b in (a, a + 1):
            if b >= tiles:
                continue
            low = w_ref[128 * a:128 * a + 128, 128 * b:128 * b + 128]
            mirror = w_ref[128 * b:128 * b + 128, 128 * a:128 * a + 128].T
            upper = (ci + 128 * b) // KDOF > (ri + 128 * a) // KDOF
            tile_val = jnp.where(upper, mirror, low)
            if a == b:
                tile_val = tile_val + jnp.where(ri == ci, damp_ref[:, 128 * a:128 * a + 128], 0.0)
            w_ref[128 * a:128 * a + 128, 128 * b:128 * b + 128] = tile_val

    rows = PANEL + band_w
    lane = lax.broadcasted_iota(jnp.int32, (rows, WIDTH), 1)
    row = lax.broadcasted_iota(jnp.int32, (rows, 1), 0)

    def panel(p, blk):
        j0 = pl.multiple_of(p * PANEL, PANEL)
        base = pl.multiple_of((p // (128 // PANEL)) * 128, 128)
        off = j0 - base
        first = blk[:, :128]
        lane_first = lane[:, :128]
        cols = [jnp.sum(jnp.where(lane_first == off + t, first, 0.0), axis=1, keepdims=True)
                for t in range(PANEL)]
        lcols = []
        invs = []
        for t in range(PANEL):
            inv = lax.rsqrt(cols[t][t:t + 1, :])
            lcol = jnp.where(row >= t, cols[t] * inv, 0.0)
            lcols.append(lcol)
            invs.append(inv)
            for t2 in range(t + 1, PANEL):
                cols[t2] = cols[t2] - lcol * lcol[t2:t2 + 1, :]
        rrows = []
        for t in range(PANEL):
            acc = blk[t:t + 1, :]
            for t1 in range(t):
                acc = acc - lcols[t1][t:t + 1, :] * rrows[t1]
            rrows.append(jnp.where(lane[0:1, :] >= off + t, acc * invs[t], 0.0))
        r_ref[pl.ds(j0, PANEL), pl.ds(base, WIDTH)] = jnp.concatenate(rrows, axis=0)
        trail = blk[PANEL:, :]
        for t in range(PANEL):
            trail = trail - lcols[t][PANEL:, :] * rrows[t]
        nxt = jnp.minimum(((p + 1) // (128 // PANEL)) * 128, w_ref.shape[1] - WIDTH)
        nxt = pl.multiple_of(nxt, 128)
        moved = jnp.concatenate([trail[:, 128:], jnp.zeros((band_w, WIDTH - 128), jnp.float32)], axis=1)
        trail = jnp.where(nxt != base, moved, trail)
        fresh = w_ref[pl.ds(pl.multiple_of(j0 + rows, PANEL), PANEL), pl.ds(nxt, WIDTH)]
        return jnp.concatenate([trail, fresh], axis=0)

    lax.fori_loop(0, n // PANEL, panel, w_ref[0:rows, 0:WIDTH])
    out_ref[...] = r_ref[0:n, 0:n]


def band_cholesky(yt, damping, n):
    band_w = yt.shape[0]
    padded = n + 128
    return pl.pallas_call(
        functools.partial(band_chol_kernel, n, band_w),
        out_shape=jax.ShapeDtypeStruct((n, n), jnp.float32),
        in_specs=[pl.BlockSpec(memory_space=pltpu.VMEM)] * 2,
        out_specs=pl.BlockSpec(memory_space=pltpu.VMEM),
        scratch_shapes=[
            pltpu.VMEM((n + 64, padded), jnp.float32),
            pltpu.VMEM((n, padded), jnp.float32),
        ],
    )(yt, damping.reshape(1, n))


def scatter_sum(band, axis):
    n = lax.axis_size(axis)
    got = lax.all_to_all(band, axis, 0, 0, tiled=True)
    got = got.reshape(n, band.shape[0] // n, band.shape[1])
    total = got[0]
    for j in range(1, n):
        total = total + got[j]
    return total


def butterfly_sum(band, axis):
    n = lax.axis_size(axis)
    s = 1
    while s < n:
        band = band + lax.ppermute(band, axis, [(i, i ^ s) for i in range(n)])
        s *= 2
    return band


def local(land_jac, pose_jac, segment, knot_frac, track_len, block_base, damping):
    num_blocks = block_base.shape[0]
    grams = block_grams_kernel(land_jac, pose_jac, segment, knot_frac, track_len, num_blocks, 8)
    group_cols = damping.shape[0]
    num_groups = lax.axis_size("cols")
    band = place_band(skew_blocks(grams), block_base, group_cols, num_groups)
    band_whole = butterfly_sum(scatter_sum(band, "cols"), "rows")
    group_knots = group_cols // KDOF
    yt = band_whole.reshape(group_knots, WIN_KNOTS, KDOF, KDOF).transpose(1, 3, 0, 2)
    yt = yt.reshape(WIN_KNOTS * KDOF, group_cols)
    return band_cholesky(yt, damping, group_cols)


def solution(mesh):
    return jax.shard_map(
        local,
        mesh=mesh,
        in_specs=(
            P(None, None, ("rows", "cols")),
            P(None, None, ("rows", "cols")),
            P(None, ("rows", "cols")),
            P(None, ("rows", "cols")),
            P(("rows", "cols")),
            P(("rows", "cols")),
            P("cols"),
        ),
        out_specs=P("cols", None),
        check_vma=False,
    )
```

```python
import jax
import jax.numpy as jnp
from jax import lax
from jax.sharding import PartitionSpec as P
from jax.experimental import pallas as pl
from jax.experimental.pallas import tpu as pltpu
import functools

KDOF = 6
WIN_KNOTS = 8
PANEL = 8
WIDTH = 256


def gram_kernel(ldim, pdim, land_ref, pose_ref, seg_ref, frac_ref, len_ref, out_ref):
    num_obs, lanes = seg_ref.shape
    rows = 2 * num_obs
    u = frac_ref[...]
    u_square = u * u
    u_cubed = u_square * u
    basis = (
        (1.0 - u) ** 3 / 6.0,
        (3.0 * u_cubed - 6.0 * u_square + 4.0) / 6.0,
        (-3.0 * u_cubed + 3.0 * u_square + 3.0 * u + 1.0) / 6.0,
        u_cubed / 6.0,
    )
    seg = seg_ref[...]
    obs = lax.broadcasted_iota(jnp.int32, (num_obs, lanes), 0)
    observed = (obs < len_ref[...]).astype(jnp.float32)
    knot = lax.broadcasted_iota(jnp.int32, (WIN_KNOTS, lanes), 0)
    land = []
    knots = []
    for j in range(num_obs):
        seg_j = seg[j:j + 1, :]
        weight = jnp.zeros((WIN_KNOTS, lanes), jnp.float32)
        for k in range(4):
            weight = weight + basis[k][j:j + 1, :] * (seg_j + k == knot).astype(jnp.float32)
        mask = observed[j:j + 1, :]
        for i in range(2):
            r = 2 * j + i
            land.append(jnp.concatenate([land_ref[c, r:r + 1, :] for c in range(ldim)], axis=0) * mask)
            knots.append(jnp.concatenate([(pose_ref[e, r:r + 1, :] * mask) * weight for e in range(KDOF)], axis=0))
    for k in range(3):
        column = [land[r][k:k + 1, :] for r in range(k, rows)]
        total = column[0] * column[0]
        for x in column[1:]:
            total = total + x * x
        length = jnp.sqrt(total)
        signum = jnp.where(column[0] >= 0.0, 1.0, -1.0)
        vector = [column[0] + signum * length] + column[1:]
        vv = vector[0] * vector[0]
        for x in vector[1:]:
            vv = vv + x * x
        scale = 2.0 / vv
        for mats in (land, knots):
            proj = vector[0] * mats[k]
            for idx in range(1, rows - k):
                proj = proj + vector[idx] * mats[k + idx]
            for idx in range(rows - k):
                mats[k + idx] = mats[k + idx] - (scale * vector[idx]) * proj
    for s in range(out_ref.shape[0]):
        reduced = jnp.concatenate([m[:, 128 * s:128 * (s + 1)] for m in knots[3:]], axis=1)
        out_ref[s] = lax.dot_general(reduced, reduced, (((1,), (1,)), ((), ())),
                                     precision=lax.Precision.HIGH, preferred_element_type=jnp.float32)


def block_grams_kernel(land_jac, pose_jac, segment, knot_frac, track_len, num_blocks, per_step=1):
    rows, ldim, landmarks = land_jac.shape
    pdim = pose_jac.shape[1]
    num_obs = segment.shape[0]
    sub = landmarks // num_blocks
    blk = sub * per_step
    width = WIN_KNOTS * KDOF
    return pl.pallas_call(
        functools.partial(gram_kernel, ldim, pdim),
        out_shape=jax.ShapeDtypeStruct((num_blocks, width, width), jnp.float32),
        grid=(num_blocks // per_step,),
        in_specs=[
            pl.BlockSpec((ldim, rows, blk), lambda b: (0, 0, b)),
            pl.BlockSpec((pdim, rows, blk), lambda b: (0, 0, b)),
            pl.BlockSpec((num_obs, blk), lambda b: (0, b)),
            pl.BlockSpec((num_obs, blk), lambda b: (0, b)),
            pl.BlockSpec((1, blk), lambda b: (0, b)),
        ],
        out_specs=pl.BlockSpec((per_step, width, width), lambda b: (b, 0, 0)),
    )(jnp.transpose(land_jac, (1, 0, 2)), jnp.transpose(pose_jac, (1, 0, 2)),
      segment, knot_frac, track_len.reshape(1, landmarks))


def skew_blocks(grams):
    num_blocks = grams.shape[0]
    g5 = grams.reshape(num_blocks, KDOF, WIN_KNOTS, KDOF, WIN_KNOTS).transpose(0, 2, 1, 4, 3)
    k1 = lax.broadcasted_iota(jnp.int32, (WIN_KNOTS, WIN_KNOTS, WIN_KNOTS), 0)
    k2 = lax.broadcasted_iota(jnp.int32, (WIN_KNOTS, WIN_KNOTS, WIN_KNOTS), 1)
    d = lax.broadcasted_iota(jnp.int32, (WIN_KNOTS, WIN_KNOTS, WIN_KNOTS), 2)
    pick = (k2 == k1 + d).astype(jnp.float32)
    return jnp.einsum("bienf,ind->bidef", g5, pick, precision=lax.Precision.HIGH)


def place_band(skewed, block_start, group_cols, num_groups):
    num_blocks = skewed.shape[0]
    group_knots = group_cols // KDOF
    rows = num_groups * group_knots
    target = (block_start // group_knots) * group_knots + block_start % group_knots
    target = target[:, None] + jnp.arange(WIN_KNOTS, dtype=jnp.int32)[None, :]
    row_id = lax.broadcasted_iota(jnp.int32, (rows, num_blocks, WIN_KNOTS), 0)
    onehot = (row_id == target[None]).astype(jnp.float32).reshape(rows, num_blocks * WIN_KNOTS)
    flat = skewed.reshape(num_blocks * WIN_KNOTS, WIN_KNOTS * KDOF * KDOF)
    return jnp.dot(onehot, flat, precision=lax.Precision.HIGH)


def band_chol_kernel(n, band_w, yt_ref, damp_ref, out_ref, w_ref, r_ref):
    w_ref[...] = jnp.zeros_like(w_ref)
    r_ref[...] = jnp.zeros_like(r_ref)
    for k in range(n // KDOF):
        lo = KDOF * k
        tile = (lo // 128) * 128
        span = 128 if lo - tile + KDOF <= 128 else WIDTH
        lanes = lax.broadcasted_iota(jnp.int32, (band_w, span), 1)
        blk = yt_ref[:, tile:tile + span]
        keep = (lanes >= lo - tile) & (lanes < lo - tile + KDOF)
        w_ref[lo:lo + band_w, tile:tile + span] += jnp.where(keep, blk, 0.0)
    tiles = n // 128
    ri = lax.broadcasted_iota(jnp.int32, (128, 128), 0)
    ci = lax.broadcasted_iota(jnp.int32, (128, 128), 1)
    for a in range(tiles):
        for b in (a, a + 1):
            if b >= tiles:
                continue
            low = w_ref[128 * a:128 * a + 128, 128 * b:128 * b + 128]
            mirror = w_ref[128 * b:128 * b + 128, 128 * a:128 * a + 128].T
            upper = (ci + 128 * b) // KDOF > (ri + 128 * a) // KDOF
            tile_val = jnp.where(upper, mirror, low)
            if a == b:
                tile_val = tile_val + jnp.where(ri == ci, damp_ref[:, 128 * a:128 * a + 128], 0.0)
            w_ref[128 * a:128 * a + 128, 128 * b:128 * b + 128] = tile_val

    rows = PANEL + band_w
    lane = lax.broadcasted_iota(jnp.int32, (rows, WIDTH), 1)
    row = lax.broadcasted_iota(jnp.int32, (rows, 1), 0)

    def panel(p, blk):
        j0 = pl.multiple_of(p * PANEL, PANEL)
        base = pl.multiple_of((p // (128 // PANEL)) * 128, 128)
        off = j0 - base
        first = blk[:, :128]
        lane_first = lane[:, :128]
        cols = [jnp.sum(jnp.where(lane_first == off + t, first, 0.0), axis=1, keepdims=True)
                for t in range(PANEL)]
        lcols = []
        invs = []
        for t in range(PANEL):
            inv = lax.rsqrt(cols[t][t:t + 1, :])
            lcol = jnp.where(row >= t, cols[t] * inv, 0.0)
            lcols.append(lcol)
            invs.append(inv)
            for t2 in range(t + 1, PANEL):
                cols[t2] = cols[t2] - lcol * lcol[t2:t2 + 1, :]
        rrows = []
        for t in range(PANEL):
            acc = blk[t:t + 1, :]
            for t1 in range(t):
                acc = acc - lcols[t1][t:t + 1, :] * rrows[t1]
            rrows.append(jnp.where(lane[0:1, :] >= off + t, acc * invs[t], 0.0))
        r_ref[pl.ds(j0, PANEL), pl.ds(base, WIDTH)] = jnp.concatenate(rrows, axis=0)
        trail = blk[PANEL:, :]
        for t in range(PANEL):
            trail = trail - lcols[t][PANEL:, :] * rrows[t]
        nxt = jnp.minimum(((p + 1) // (128 // PANEL)) * 128, w_ref.shape[1] - WIDTH)
        nxt = pl.multiple_of(nxt, 128)
        moved = jnp.concatenate([trail[:, 128:], jnp.zeros((band_w, WIDTH - 128), jnp.float32)], axis=1)
        trail = jnp.where(nxt != base, moved, trail)
        fresh = w_ref[pl.ds(pl.multiple_of(j0 + rows, PANEL), PANEL), pl.ds(nxt, WIDTH)]
        return jnp.concatenate([trail, fresh], axis=0)

    lax.fori_loop(0, n // PANEL, panel, w_ref[0:rows, 0:WIDTH])
    out_ref[...] = r_ref[0:n, 0:n]


def band_cholesky(yt, damping, n):
    band_w = yt.shape[0]
    padded = n + 128
    return pl.pallas_call(
        functools.partial(band_chol_kernel, n, band_w),
        out_shape=jax.ShapeDtypeStruct((n, n), jnp.float32),
        in_specs=[pl.BlockSpec(memory_space=pltpu.VMEM)] * 2,
        out_specs=pl.BlockSpec(memory_space=pltpu.VMEM),
        scratch_shapes=[
            pltpu.VMEM((n + 64, padded), jnp.float32),
            pltpu.VMEM((n, padded), jnp.float32),
        ],
    )(yt, damping.reshape(1, n))


def scatter_sum(band, axis):
    n = lax.axis_size(axis)
    got = lax.all_to_all(band, axis, 0, 0, tiled=True)
    got = got.reshape(n, band.shape[0] // n, band.shape[1])
    total = got[0]
    for j in range(1, n):
        total = total + got[j]
    return total


def butterfly_sum(band, axis):
    n = lax.axis_size(axis)
    s = 1
    while s < n:
        band = band + lax.ppermute(band, axis, [(i, i ^ s) for i in range(n)])
        s *= 2
    return band


def local(land_jac, pose_jac, segment, knot_frac, track_len, block_base, damping):
    num_blocks = block_base.shape[0]
    grams = block_grams_kernel(land_jac, pose_jac, segment, knot_frac, track_len, num_blocks, 8)
    group_cols = damping.shape[0]
    num_groups = lax.axis_size("cols")
    band = place_band(skew_blocks(grams), block_base, group_cols, num_groups)
    band_whole = butterfly_sum(scatter_sum(band, "cols"), "rows")
    group_knots = group_cols // KDOF
    yt = band_whole.reshape(group_knots, WIN_KNOTS, KDOF, KDOF).transpose(1, 3, 0, 2)
    yt = yt.reshape(WIN_KNOTS * KDOF, group_cols)
    return band_cholesky(yt, damping, group_cols)


def solution(mesh):
    return jax.shard_map(
        local,
        mesh=mesh,
        in_specs=(
            P(None, None, ("rows", "cols")),
            P(None, None, ("rows", "cols")),
            P(None, ("rows", "cols")),
            P(None, ("rows", "cols")),
            P(("rows", "cols")),
            P(("rows", "cols")),
            P("cols"),
        ),
        out_specs=P("cols", None),
        check_vma=False,
    )
```

```python
import jax
import jax.numpy as jnp
from jax import lax
from jax.sharding import PartitionSpec as P
from jax.experimental import pallas as pl
from jax.experimental.pallas import tpu as pltpu
import functools

KDOF = 6
WIN_KNOTS = 8
PANEL = 8
WIDTH = 256


def gram_kernel(ldim, pdim, land_ref, pose_ref, seg_ref, frac_ref, len_ref, out_ref):
    num_obs, lanes = seg_ref.shape
    rows = 2 * num_obs
    u = frac_ref[...]
    u_square = u * u
    u_cubed = u_square * u
    basis = (
        (1.0 - u) ** 3 / 6.0,
        (3.0 * u_cubed - 6.0 * u_square + 4.0) / 6.0,
        (-3.0 * u_cubed + 3.0 * u_square + 3.0 * u + 1.0) / 6.0,
        u_cubed / 6.0,
    )
    seg = seg_ref[...]
    obs = lax.broadcasted_iota(jnp.int32, (num_obs, lanes), 0)
    observed = (obs < len_ref[...]).astype(jnp.float32)
    knot = lax.broadcasted_iota(jnp.int32, (WIN_KNOTS, lanes), 0)
    land = []
    knots = []
    for j in range(num_obs):
        seg_j = seg[j:j + 1, :]
        weight = jnp.zeros((WIN_KNOTS, lanes), jnp.float32)
        for k in range(4):
            weight = weight + basis[k][j:j + 1, :] * (seg_j + k == knot).astype(jnp.float32)
        mask = observed[j:j + 1, :]
        for i in range(2):
            r = 2 * j + i
            land.append(jnp.concatenate([land_ref[c, r:r + 1, :] for c in range(ldim)], axis=0) * mask)
            knots.append(jnp.concatenate([(pose_ref[e, r:r + 1, :] * mask) * weight for e in range(KDOF)], axis=0))
    for k in range(3):
        column = [land[r][k:k + 1, :] for r in range(k, rows)]
        total = column[0] * column[0]
        for x in column[1:]:
            total = total + x * x
        length = jnp.sqrt(total)
        signum = jnp.where(column[0] >= 0.0, 1.0, -1.0)
        vector = [column[0] + signum * length] + column[1:]
        vv = vector[0] * vector[0]
        for x in vector[1:]:
            vv = vv + x * x
        scale = 2.0 / vv
        for mats in (land, knots):
            proj = vector[0] * mats[k]
            for idx in range(1, rows - k):
                proj = proj + vector[idx] * mats[k + idx]
            for idx in range(rows - k):
                mats[k + idx] = mats[k + idx] - (scale * vector[idx]) * proj
    for s in range(out_ref.shape[0]):
        reduced = jnp.concatenate([m[:, 128 * s:128 * (s + 1)] for m in knots[3:]], axis=1)
        out_ref[s] = lax.dot_general(reduced, reduced, (((1,), (1,)), ((), ())),
                                     precision=lax.Precision.HIGH, preferred_element_type=jnp.float32)


def block_grams_kernel(land_jac, pose_jac, segment, knot_frac, track_len, num_blocks, per_step=1):
    rows, ldim, landmarks = land_jac.shape
    pdim = pose_jac.shape[1]
    num_obs = segment.shape[0]
    sub = landmarks // num_blocks
    blk = sub * per_step
    width = WIN_KNOTS * KDOF
    return pl.pallas_call(
        functools.partial(gram_kernel, ldim, pdim),
        out_shape=jax.ShapeDtypeStruct((num_blocks, width, width), jnp.float32),
        grid=(num_blocks // per_step,),
        in_specs=[
            pl.BlockSpec((ldim, rows, blk), lambda b: (0, 0, b)),
            pl.BlockSpec((pdim, rows, blk), lambda b: (0, 0, b)),
            pl.BlockSpec((num_obs, blk), lambda b: (0, b)),
            pl.BlockSpec((num_obs, blk), lambda b: (0, b)),
            pl.BlockSpec((1, blk), lambda b: (0, b)),
        ],
        out_specs=pl.BlockSpec((per_step, width, width), lambda b: (b, 0, 0)),
    )(jnp.transpose(land_jac, (1, 0, 2)), jnp.transpose(pose_jac, (1, 0, 2)),
      segment, knot_frac, track_len.reshape(1, landmarks))


def skew_blocks(grams):
    num_blocks = grams.shape[0]
    g5 = grams.reshape(num_blocks, KDOF, WIN_KNOTS, KDOF, WIN_KNOTS).transpose(0, 2, 1, 4, 3)
    k1 = lax.broadcasted_iota(jnp.int32, (WIN_KNOTS, WIN_KNOTS, WIN_KNOTS), 0)
    k2 = lax.broadcasted_iota(jnp.int32, (WIN_KNOTS, WIN_KNOTS, WIN_KNOTS), 1)
    d = lax.broadcasted_iota(jnp.int32, (WIN_KNOTS, WIN_KNOTS, WIN_KNOTS), 2)
    pick = (k2 == k1 + d).astype(jnp.float32)
    return jnp.einsum("bienf,ind->bidef", g5, pick, precision=lax.Precision.HIGH)


def place_band(skewed, block_start, group_cols, num_groups):
    num_blocks = skewed.shape[0]
    group_knots = group_cols // KDOF
    rows = num_groups * group_knots
    target = (block_start // group_knots) * group_knots + block_start % group_knots
    target = target[:, None] + jnp.arange(WIN_KNOTS, dtype=jnp.int32)[None, :]
    row_id = lax.broadcasted_iota(jnp.int32, (rows, num_blocks, WIN_KNOTS), 0)
    onehot = (row_id == target[None]).astype(jnp.float32).reshape(rows, num_blocks * WIN_KNOTS)
    flat = skewed.reshape(num_blocks * WIN_KNOTS, WIN_KNOTS * KDOF * KDOF)
    return jnp.dot(onehot, flat, precision=lax.Precision.HIGH)


def band_chol_kernel(n, band_w, yt_ref, damp_ref, out_ref, w_ref):
    w_ref[...] = jnp.zeros_like(w_ref)
    out_ref[...] = jnp.zeros_like(out_ref)
    for k in range(n // KDOF):
        lo = KDOF * k
        tile = (lo // 128) * 128
        span = 128 if lo - tile + KDOF <= 128 else WIDTH
        lanes = lax.broadcasted_iota(jnp.int32, (band_w, span), 1)
        blk = yt_ref[:, tile:tile + span]
        keep = (lanes >= lo - tile) & (lanes < lo - tile + KDOF)
        w_ref[lo:lo + band_w, tile:tile + span] += jnp.where(keep, blk, 0.0)
    tiles = n // 128
    ri = lax.broadcasted_iota(jnp.int32, (128, 128), 0)
    ci = lax.broadcasted_iota(jnp.int32, (128, 128), 1)
    for a in range(tiles):
        for b in (a, a + 1):
            if b >= tiles:
                continue
            low = w_ref[128 * a:128 * a + 128, 128 * b:128 * b + 128]
            mirror = w_ref[128 * b:128 * b + 128, 128 * a:128 * a + 128].T
            upper = (ci + 128 * b) // KDOF > (ri + 128 * a) // KDOF
            tile_val = jnp.where(upper, mirror, low)
            if a == b:
                tile_val = tile_val + jnp.where(ri == ci, damp_ref[:, 128 * a:128 * a + 128], 0.0)
            w_ref[128 * a:128 * a + 128, 128 * b:128 * b + 128] = tile_val

    rows = PANEL + band_w
    lane = lax.broadcasted_iota(jnp.int32, (rows, WIDTH), 1)
    row = lax.broadcasted_iota(jnp.int32, (rows, 1), 0)

    def panel(p, blk):
        j0 = pl.multiple_of(p * PANEL, PANEL)
        base = pl.multiple_of((p // (128 // PANEL)) * 128, 128)
        off = j0 - base
        first = blk[:, :128]
        lane_first = lane[:, :128]
        cols = [jnp.sum(jnp.where(lane_first == off + t, first, 0.0), axis=1, keepdims=True)
                for t in range(PANEL)]
        lcols = []
        invs = []
        for t in range(PANEL):
            inv = lax.rsqrt(cols[t][t:t + 1, :])
            lcol = jnp.where(row >= t, cols[t] * inv, 0.0)
            lcols.append(lcol)
            invs.append(inv)
            for t2 in range(t + 1, PANEL):
                cols[t2] = cols[t2] - lcol * lcol[t2:t2 + 1, :]
        rrows = []
        for t in range(PANEL):
            acc = blk[t:t + 1, :]
            for t1 in range(t):
                acc = acc - lcols[t1][t:t + 1, :] * rrows[t1]
            rrows.append(jnp.where(lane[0:1, :] >= off + t, acc * invs[t], 0.0))
        rp = jnp.concatenate(rrows, axis=0)
        last = n - 128

        @pl.when(base < last)
        def _():
            out_ref[pl.ds(j0, PANEL), pl.ds(base, WIDTH)] = rp

        @pl.when(base >= last)
        def _():
            out_ref[pl.ds(j0, PANEL), pl.ds(last, 128)] = rp[:, :128]
        trail = blk[PANEL:, :]
        for t in range(PANEL):
            trail = trail - lcols[t][PANEL:, :] * rrows[t]
        nxt = jnp.minimum(((p + 1) // (128 // PANEL)) * 128, w_ref.shape[1] - WIDTH)
        nxt = pl.multiple_of(nxt, 128)
        moved = jnp.concatenate([trail[:, 128:], jnp.zeros((band_w, WIDTH - 128), jnp.float32)], axis=1)
        trail = jnp.where(nxt != base, moved, trail)
        fresh = w_ref[pl.ds(pl.multiple_of(j0 + rows, PANEL), PANEL), pl.ds(nxt, WIDTH)]
        return jnp.concatenate([trail, fresh], axis=0)

    lax.fori_loop(0, n // PANEL, panel, w_ref[0:rows, 0:WIDTH])


def band_cholesky(yt, damping, n):
    band_w = yt.shape[0]
    padded = n + 128
    return pl.pallas_call(
        functools.partial(band_chol_kernel, n, band_w),
        out_shape=jax.ShapeDtypeStruct((n, n), jnp.float32),
        in_specs=[pl.BlockSpec(memory_space=pltpu.VMEM)] * 2,
        out_specs=pl.BlockSpec(memory_space=pltpu.VMEM),
        scratch_shapes=[
            pltpu.VMEM((n + 64, padded), jnp.float32),
        ],
    )(yt, damping.reshape(1, n))


def scatter_sum(band, axis):
    n = lax.axis_size(axis)
    got = lax.all_to_all(band, axis, 0, 0, tiled=True)
    got = got.reshape(n, band.shape[0] // n, band.shape[1])
    total = got[0]
    for j in range(1, n):
        total = total + got[j]
    return total


def butterfly_sum(band, axis):
    n = lax.axis_size(axis)
    s = 1
    while s < n:
        band = band + lax.ppermute(band, axis, [(i, i ^ s) for i in range(n)])
        s *= 2
    return band


def local(land_jac, pose_jac, segment, knot_frac, track_len, block_base, damping):
    num_blocks = block_base.shape[0]
    grams = block_grams_kernel(land_jac, pose_jac, segment, knot_frac, track_len, num_blocks, 8)
    group_cols = damping.shape[0]
    num_groups = lax.axis_size("cols")
    band = place_band(skew_blocks(grams), block_base, group_cols, num_groups)
    band_whole = butterfly_sum(scatter_sum(band, "cols"), "rows")
    group_knots = group_cols // KDOF
    yt = band_whole.reshape(group_knots, WIN_KNOTS, KDOF, KDOF).transpose(1, 3, 0, 2)
    yt = yt.reshape(WIN_KNOTS * KDOF, group_cols)
    return band_cholesky(yt, damping, group_cols)


def solution(mesh):
    return jax.shard_map(
        local,
        mesh=mesh,
        in_specs=(
            P(None, None, ("rows", "cols")),
            P(None, None, ("rows", "cols")),
            P(None, ("rows", "cols")),
            P(None, ("rows", "cols")),
            P(("rows", "cols")),
            P(("rows", "cols")),
            P("cols"),
        ),
        out_specs=P("cols", None),
        check_vma=False,
    )
```

```python
import jax
import jax.numpy as jnp
from jax import lax
from jax.sharding import PartitionSpec as P
from jax.experimental import pallas as pl
from jax.experimental.pallas import tpu as pltpu
import functools

KDOF = 6
WIN_KNOTS = 8
PANEL = 8
WIDTH = 256


def gram_kernel(ldim, pdim, land_ref, pose_ref, seg_ref, frac_ref, len_ref, out_ref):
    num_obs, lanes = seg_ref.shape
    rows = 2 * num_obs
    u = frac_ref[...]
    u_square = u * u
    u_cubed = u_square * u
    basis = (
        (1.0 - u) ** 3 / 6.0,
        (3.0 * u_cubed - 6.0 * u_square + 4.0) / 6.0,
        (-3.0 * u_cubed + 3.0 * u_square + 3.0 * u + 1.0) / 6.0,
        u_cubed / 6.0,
    )
    seg = seg_ref[...]
    obs = lax.broadcasted_iota(jnp.int32, (num_obs, lanes), 0)
    observed = (obs < len_ref[...]).astype(jnp.float32)
    knot = lax.broadcasted_iota(jnp.int32, (WIN_KNOTS, lanes), 0)
    land = []
    knots = []
    for j in range(num_obs):
        seg_j = seg[j:j + 1, :]
        weight = jnp.zeros((WIN_KNOTS, lanes), jnp.float32)
        for k in range(4):
            weight = weight + basis[k][j:j + 1, :] * (seg_j + k == knot).astype(jnp.float32)
        mask = observed[j:j + 1, :]
        for i in range(2):
            r = 2 * j + i
            land.append(jnp.concatenate([land_ref[c, r:r + 1, :] for c in range(ldim)], axis=0) * mask)
            knots.append(jnp.concatenate([(pose_ref[e, r:r + 1, :] * mask) * weight for e in range(KDOF)], axis=0))
    for k in range(3):
        column = [land[r][k:k + 1, :] for r in range(k, rows)]
        total = column[0] * column[0]
        for x in column[1:]:
            total = total + x * x
        length = jnp.sqrt(total)
        signum = jnp.where(column[0] >= 0.0, 1.0, -1.0)
        vector = [column[0] + signum * length] + column[1:]
        vv = vector[0] * vector[0]
        for x in vector[1:]:
            vv = vv + x * x
        scale = 2.0 / vv
        for mats in (land, knots):
            proj = vector[0] * mats[k]
            for idx in range(1, rows - k):
                proj = proj + vector[idx] * mats[k + idx]
            for idx in range(rows - k):
                mats[k + idx] = mats[k + idx] - (scale * vector[idx]) * proj
    for s in range(out_ref.shape[0]):
        reduced = jnp.concatenate([m[:, 128 * s:128 * (s + 1)] for m in knots[3:]], axis=1)
        out_ref[s] = lax.dot_general(reduced, reduced, (((1,), (1,)), ((), ())),
                                     precision=lax.Precision.HIGH, preferred_element_type=jnp.float32)


def block_grams_kernel(land_jac, pose_jac, segment, knot_frac, track_len, num_blocks, per_step=1):
    rows, ldim, landmarks = land_jac.shape
    pdim = pose_jac.shape[1]
    num_obs = segment.shape[0]
    sub = landmarks // num_blocks
    blk = sub * per_step
    width = WIN_KNOTS * KDOF
    return pl.pallas_call(
        functools.partial(gram_kernel, ldim, pdim),
        out_shape=jax.ShapeDtypeStruct((num_blocks, width, width), jnp.float32),
        grid=(num_blocks // per_step,),
        in_specs=[
            pl.BlockSpec((ldim, rows, blk), lambda b: (0, 0, b)),
            pl.BlockSpec((pdim, rows, blk), lambda b: (0, 0, b)),
            pl.BlockSpec((num_obs, blk), lambda b: (0, b)),
            pl.BlockSpec((num_obs, blk), lambda b: (0, b)),
            pl.BlockSpec((1, blk), lambda b: (0, b)),
        ],
        out_specs=pl.BlockSpec((per_step, width, width), lambda b: (b, 0, 0)),
    )(jnp.transpose(land_jac, (1, 0, 2)), jnp.transpose(pose_jac, (1, 0, 2)),
      segment, knot_frac, track_len.reshape(1, landmarks))


def skew_blocks(grams):
    num_blocks = grams.shape[0]
    g5 = grams.reshape(num_blocks, KDOF, WIN_KNOTS, KDOF, WIN_KNOTS).transpose(0, 2, 1, 4, 3)
    k1 = lax.broadcasted_iota(jnp.int32, (WIN_KNOTS, WIN_KNOTS, WIN_KNOTS), 0)
    k2 = lax.broadcasted_iota(jnp.int32, (WIN_KNOTS, WIN_KNOTS, WIN_KNOTS), 1)
    d = lax.broadcasted_iota(jnp.int32, (WIN_KNOTS, WIN_KNOTS, WIN_KNOTS), 2)
    pick = (k2 == k1 + d).astype(jnp.float32)
    return jnp.einsum("bienf,ind->bidef", g5, pick, precision=lax.Precision.HIGH)


def place_band(skewed, block_start, group_cols, num_groups):
    num_blocks = skewed.shape[0]
    group_knots = group_cols // KDOF
    rows = num_groups * group_knots
    target = (block_start // group_knots) * group_knots + block_start % group_knots
    target = target[:, None] + jnp.arange(WIN_KNOTS, dtype=jnp.int32)[None, :]
    row_id = lax.broadcasted_iota(jnp.int32, (rows, num_blocks, WIN_KNOTS), 0)
    onehot = (row_id == target[None]).astype(jnp.float32).reshape(rows, num_blocks * WIN_KNOTS)
    flat = skewed.reshape(num_blocks * WIN_KNOTS, WIN_KNOTS * KDOF * KDOF)
    return jnp.dot(onehot, flat, precision=lax.Precision.HIGH)


def band_chol_kernel(n, band_w, yt_ref, damp_ref, out_ref, w_ref, r_ref):
    w_ref[...] = jnp.zeros_like(w_ref)
    r_ref[...] = jnp.zeros_like(r_ref)
    for k in range(n // KDOF):
        lo = KDOF * k
        tile = (lo // 128) * 128
        span = 128 if lo - tile + KDOF <= 128 else WIDTH
        lanes = lax.broadcasted_iota(jnp.int32, (band_w, span), 1)
        blk = yt_ref[:, tile:tile + span]
        keep = (lanes >= lo - tile) & (lanes < lo - tile + KDOF)
        w_ref[lo:lo + band_w, tile:tile + span] += jnp.where(keep, blk, 0.0)
    tiles = n // 128
    ri = lax.broadcasted_iota(jnp.int32, (128, 128), 0)
    ci = lax.broadcasted_iota(jnp.int32, (128, 128), 1)
    for a in range(tiles):
        for b in (a, a + 1):
            if b >= tiles:
                continue
            low = w_ref[128 * a:128 * a + 128, 128 * b:128 * b + 128]
            mirror = w_ref[128 * b:128 * b + 128, 128 * a:128 * a + 128].T
            upper = (ci + 128 * b) // KDOF > (ri + 128 * a) // KDOF
            tile_val = jnp.where(upper, mirror, low)
            if a == b:
                tile_val = tile_val + jnp.where(ri == ci, damp_ref[:, 128 * a:128 * a + 128], 0.0)
            w_ref[128 * a:128 * a + 128, 128 * b:128 * b + 128] = tile_val

    rows = PANEL + band_w
    lane = lax.broadcasted_iota(jnp.int32, (rows, WIDTH), 1)
    row = lax.broadcasted_iota(jnp.int32, (rows, 1), 0)

    def panel(p, blk):
        j0 = pl.multiple_of(p * PANEL, PANEL)
        base = pl.multiple_of((p // (128 // PANEL)) * 128, 128)
        off = j0 - base
        first = blk[:, :128]
        lane_first = lane[:, :128]
        cols = [jnp.sum(jnp.where(lane_first == off + t, first, 0.0), axis=1, keepdims=True)
                for t in range(PANEL)]
        lcols = []
        invs = []
        for t in range(PANEL):
            inv = lax.rsqrt(cols[t][t:t + 1, :])
            lcol = jnp.where(row >= t, cols[t] * inv, 0.0)
            lcols.append(lcol)
            invs.append(inv)
            for t2 in range(t + 1, PANEL):
                cols[t2] = cols[t2] - lcol * lcol[t2:t2 + 1, :]
        rrows = []
        for t in range(PANEL):
            acc = blk[t:t + 1, :]
            for t1 in range(t):
                acc = acc - lcols[t1][t:t + 1, :] * rrows[t1]
            rrows.append(jnp.where(lane[0:1, :] >= off + t, acc * invs[t], 0.0))
        r_ref[pl.ds(j0, PANEL), pl.ds(base, WIDTH)] = jnp.concatenate(rrows, axis=0)
        trail = blk[PANEL:, :]
        for t in range(PANEL):
            trail = trail - lcols[t][PANEL:, :] * rrows[t]
        nxt = jnp.minimum(((p + 1) // (128 // PANEL)) * 128, w_ref.shape[1] - WIDTH)
        nxt = pl.multiple_of(nxt, 128)
        moved = jnp.concatenate([trail[:, 128:], jnp.zeros((band_w, WIDTH - 128), jnp.float32)], axis=1)
        trail = jnp.where(nxt != base, moved, trail)
        fresh = w_ref[pl.ds(pl.multiple_of(j0 + rows, PANEL), PANEL), pl.ds(nxt, WIDTH)]
        return jnp.concatenate([trail, fresh], axis=0)

    lax.fori_loop(0, n // PANEL, panel, w_ref[0:rows, 0:WIDTH])
    out_ref[...] = r_ref[0:n, 0:n]


def band_cholesky(yt, damping, n):
    band_w = yt.shape[0]
    padded = n + 128
    return pl.pallas_call(
        functools.partial(band_chol_kernel, n, band_w),
        out_shape=jax.ShapeDtypeStruct((n, n), jnp.float32),
        in_specs=[pl.BlockSpec(memory_space=pltpu.VMEM)] * 2,
        out_specs=pl.BlockSpec(memory_space=pltpu.VMEM),
        scratch_shapes=[
            pltpu.VMEM((n + 64, padded), jnp.float32),
            pltpu.VMEM((n, padded), jnp.float32),
        ],
    )(yt, damping.reshape(1, n))


def scatter_sum(band, axis):
    n = lax.axis_size(axis)
    got = lax.all_to_all(band, axis, 0, 0, tiled=True)
    got = got.reshape(n, band.shape[0] // n, band.shape[1])
    total = got[0]
    for j in range(1, n):
        total = total + got[j]
    return total


def butterfly_sum(band, axis):
    n = lax.axis_size(axis)
    s = 1
    while s < n:
        band = band + lax.ppermute(band, axis, [(i, i ^ s) for i in range(n)])
        s *= 2
    return band


def local(land_jac, pose_jac, segment, knot_frac, track_len, block_base, damping):
    num_blocks = block_base.shape[0]
    grams = block_grams_kernel(land_jac, pose_jac, segment, knot_frac, track_len, num_blocks, 16)
    group_cols = damping.shape[0]
    num_groups = lax.axis_size("cols")
    band = place_band(skew_blocks(grams), block_base, group_cols, num_groups)
    band_whole = butterfly_sum(scatter_sum(band, "cols"), "rows")
    group_knots = group_cols // KDOF
    yt = band_whole.reshape(group_knots, WIN_KNOTS, KDOF, KDOF).transpose(1, 3, 0, 2)
    yt = yt.reshape(WIN_KNOTS * KDOF, group_cols)
    return band_cholesky(yt, damping, group_cols)


def solution(mesh):
    return jax.shard_map(
        local,
        mesh=mesh,
        in_specs=(
            P(None, None, ("rows", "cols")),
            P(None, None, ("rows", "cols")),
            P(None, ("rows", "cols")),
            P(None, ("rows", "cols")),
            P(("rows", "cols")),
            P(("rows", "cols")),
            P("cols"),
        ),
        out_specs=P("cols", None),
        check_vma=False,
    )
```

```python
import jax
import jax.numpy as jnp
from jax import lax
from jax.sharding import PartitionSpec as P
from jax.experimental import pallas as pl
from jax.experimental.pallas import tpu as pltpu
import functools

KDOF = 6
WIN_KNOTS = 8
PANEL = 8
WIDTH = 256


def gram_kernel(ldim, pdim, land_ref, pose_ref, seg_ref, frac_ref, len_ref, out_ref):
    num_obs, lanes = seg_ref.shape
    rows = 2 * num_obs
    u = frac_ref[...]
    u_square = u * u
    u_cubed = u_square * u
    basis = (
        (1.0 - u) ** 3 / 6.0,
        (3.0 * u_cubed - 6.0 * u_square + 4.0) / 6.0,
        (-3.0 * u_cubed + 3.0 * u_square + 3.0 * u + 1.0) / 6.0,
        u_cubed / 6.0,
    )
    seg = seg_ref[...]
    obs = lax.broadcasted_iota(jnp.int32, (num_obs, lanes), 0)
    observed = (obs < len_ref[...]).astype(jnp.float32)
    knot = lax.broadcasted_iota(jnp.int32, (WIN_KNOTS, lanes), 0)
    land = []
    knots = []
    for j in range(num_obs):
        seg_j = seg[j:j + 1, :]
        weight = jnp.zeros((WIN_KNOTS, lanes), jnp.float32)
        for k in range(4):
            weight = weight + basis[k][j:j + 1, :] * (seg_j + k == knot).astype(jnp.float32)
        mask = observed[j:j + 1, :]
        for i in range(2):
            r = 2 * j + i
            land.append(jnp.concatenate([land_ref[c, r:r + 1, :] for c in range(ldim)], axis=0) * mask)
            knots.append(jnp.concatenate([(pose_ref[e, r:r + 1, :] * mask) * weight for e in range(KDOF)], axis=0))
    for k in range(3):
        column = [land[r][k:k + 1, :] for r in range(k, rows)]
        total = column[0] * column[0]
        for x in column[1:]:
            total = total + x * x
        length = jnp.sqrt(total)
        signum = jnp.where(column[0] >= 0.0, 1.0, -1.0)
        vector = [column[0] + signum * length] + column[1:]
        vv = vector[0] * vector[0]
        for x in vector[1:]:
            vv = vv + x * x
        scale = 2.0 / vv
        for mats in (land, knots):
            proj = vector[0] * mats[k]
            for idx in range(1, rows - k):
                proj = proj + vector[idx] * mats[k + idx]
            for idx in range(rows - k):
                mats[k + idx] = mats[k + idx] - (scale * vector[idx]) * proj
    for s in range(out_ref.shape[0]):
        reduced = jnp.concatenate([m[:, 128 * s:128 * (s + 1)] for m in knots[3:]], axis=1)
        out_ref[s] = lax.dot_general(reduced, reduced, (((1,), (1,)), ((), ())),
                                     precision=lax.Precision.HIGH, preferred_element_type=jnp.float32)


def block_grams_kernel(land_jac, pose_jac, segment, knot_frac, track_len, num_blocks, per_step=1):
    rows, ldim, landmarks = land_jac.shape
    pdim = pose_jac.shape[1]
    num_obs = segment.shape[0]
    sub = landmarks // num_blocks
    blk = sub * per_step
    width = WIN_KNOTS * KDOF
    return pl.pallas_call(
        functools.partial(gram_kernel, ldim, pdim),
        out_shape=jax.ShapeDtypeStruct((num_blocks, width, width), jnp.float32),
        grid=(num_blocks // per_step,),
        in_specs=[
            pl.BlockSpec((ldim, rows, blk), lambda b: (0, 0, b)),
            pl.BlockSpec((pdim, rows, blk), lambda b: (0, 0, b)),
            pl.BlockSpec((num_obs, blk), lambda b: (0, b)),
            pl.BlockSpec((num_obs, blk), lambda b: (0, b)),
            pl.BlockSpec((1, blk), lambda b: (0, b)),
        ],
        out_specs=pl.BlockSpec((per_step, width, width), lambda b: (b, 0, 0)),
    )(jnp.transpose(land_jac, (1, 0, 2)), jnp.transpose(pose_jac, (1, 0, 2)),
      segment, knot_frac, track_len.reshape(1, landmarks))


def skew_blocks(grams):
    num_blocks = grams.shape[0]
    g5 = grams.reshape(num_blocks, KDOF, WIN_KNOTS, KDOF, WIN_KNOTS).transpose(0, 2, 1, 4, 3)
    k1 = lax.broadcasted_iota(jnp.int32, (WIN_KNOTS, WIN_KNOTS, WIN_KNOTS), 0)
    k2 = lax.broadcasted_iota(jnp.int32, (WIN_KNOTS, WIN_KNOTS, WIN_KNOTS), 1)
    d = lax.broadcasted_iota(jnp.int32, (WIN_KNOTS, WIN_KNOTS, WIN_KNOTS), 2)
    pick = (k2 == k1 + d).astype(jnp.float32)
    return jnp.einsum("bienf,ind->bidfe", g5, pick, precision=lax.Precision.HIGH)


def place_band(skewed, block_start, group_cols, num_groups):
    num_blocks = skewed.shape[0]
    group_knots = group_cols // KDOF
    rows = num_groups * group_knots
    target = (block_start // group_knots) * group_knots + block_start % group_knots
    target = target[:, None] + jnp.arange(WIN_KNOTS, dtype=jnp.int32)[None, :]
    row_id = lax.broadcasted_iota(jnp.int32, (rows, num_blocks, WIN_KNOTS), 0)
    onehot = (row_id == target[None]).astype(jnp.float32).reshape(rows, num_blocks * WIN_KNOTS)
    flat = skewed.reshape(num_blocks * WIN_KNOTS, WIN_KNOTS * KDOF * KDOF)
    return jnp.dot(onehot, flat, precision=lax.Precision.HIGH)


def band_chol_kernel(n, band_w, yt_ref, damp_ref, out_ref, w_ref, r_ref):
    w_ref[...] = jnp.zeros_like(w_ref)
    r_ref[...] = jnp.zeros_like(r_ref)
    for k in range(n // KDOF):
        lo = KDOF * k
        tile = (lo // 128) * 128
        span = 128 if lo - tile + KDOF <= 128 else WIDTH
        lanes = lax.broadcasted_iota(jnp.int32, (band_w, span), 1)
        blk = yt_ref[:, tile:tile + span]
        keep = (lanes >= lo - tile) & (lanes < lo - tile + KDOF)
        w_ref[lo:lo + band_w, tile:tile + span] += jnp.where(keep, blk, 0.0)
    tiles = n // 128
    ri = lax.broadcasted_iota(jnp.int32, (128, 128), 0)
    ci = lax.broadcasted_iota(jnp.int32, (128, 128), 1)
    for a in range(tiles):
        for b in (a, a + 1):
            if b >= tiles:
                continue
            low = w_ref[128 * a:128 * a + 128, 128 * b:128 * b + 128]
            mirror = w_ref[128 * b:128 * b + 128, 128 * a:128 * a + 128].T
            upper = (ci + 128 * b) // KDOF > (ri + 128 * a) // KDOF
            tile_val = jnp.where(upper, mirror, low)
            if a == b:
                tile_val = tile_val + jnp.where(ri == ci, damp_ref[:, 128 * a:128 * a + 128], 0.0)
            w_ref[128 * a:128 * a + 128, 128 * b:128 * b + 128] = tile_val

    rows = PANEL + band_w
    lane = lax.broadcasted_iota(jnp.int32, (rows, WIDTH), 1)
    row = lax.broadcasted_iota(jnp.int32, (rows, 1), 0)

    def panel(p, blk):
        j0 = pl.multiple_of(p * PANEL, PANEL)
        base = pl.multiple_of((p // (128 // PANEL)) * 128, 128)
        off = j0 - base
        first = blk[:, :128]
        lane_first = lane[:, :128]
        cols = [jnp.sum(jnp.where(lane_first == off + t, first, 0.0), axis=1, keepdims=True)
                for t in range(PANEL)]
        lcols = []
        invs = []
        for t in range(PANEL):
            inv = lax.rsqrt(cols[t][t:t + 1, :])
            lcol = jnp.where(row >= t, cols[t] * inv, 0.0)
            lcols.append(lcol)
            invs.append(inv)
            for t2 in range(t + 1, PANEL):
                cols[t2] = cols[t2] - lcol * lcol[t2:t2 + 1, :]
        rrows = []
        for t in range(PANEL):
            acc = blk[t:t + 1, :]
            for t1 in range(t):
                acc = acc - lcols[t1][t:t + 1, :] * rrows[t1]
            rrows.append(jnp.where(lane[0:1, :] >= off + t, acc * invs[t], 0.0))
        r_ref[pl.ds(j0, PANEL), pl.ds(base, WIDTH)] = jnp.concatenate(rrows, axis=0)
        trail = blk[PANEL:, :]
        for t in range(PANEL):
            trail = trail - lcols[t][PANEL:, :] * rrows[t]
        nxt = jnp.minimum(((p + 1) // (128 // PANEL)) * 128, w_ref.shape[1] - WIDTH)
        nxt = pl.multiple_of(nxt, 128)
        moved = jnp.concatenate([trail[:, 128:], jnp.zeros((band_w, WIDTH - 128), jnp.float32)], axis=1)
        trail = jnp.where(nxt != base, moved, trail)
        fresh = w_ref[pl.ds(pl.multiple_of(j0 + rows, PANEL), PANEL), pl.ds(nxt, WIDTH)]
        return jnp.concatenate([trail, fresh], axis=0)

    lax.fori_loop(0, n // PANEL, panel, w_ref[0:rows, 0:WIDTH])
    out_ref[...] = r_ref[0:n, 0:n]


def band_cholesky(yt, damping, n):
    band_w = yt.shape[0]
    padded = n + 128
    return pl.pallas_call(
        functools.partial(band_chol_kernel, n, band_w),
        out_shape=jax.ShapeDtypeStruct((n, n), jnp.float32),
        in_specs=[pl.BlockSpec(memory_space=pltpu.VMEM)] * 2,
        out_specs=pl.BlockSpec(memory_space=pltpu.VMEM),
        scratch_shapes=[
            pltpu.VMEM((n + 64, padded), jnp.float32),
            pltpu.VMEM((n, padded), jnp.float32),
        ],
    )(yt, damping.reshape(1, n))


def scatter_sum(band, axis):
    n = lax.axis_size(axis)
    got = lax.all_to_all(band, axis, 0, 0, tiled=True)
    got = got.reshape(n, band.shape[0] // n, band.shape[1])
    total = got[0]
    for j in range(1, n):
        total = total + got[j]
    return total


def butterfly_sum(band, axis):
    n = lax.axis_size(axis)
    s = 1
    while s < n:
        band = band + lax.ppermute(band, axis, [(i, i ^ s) for i in range(n)])
        s *= 2
    return band


def local(land_jac, pose_jac, segment, knot_frac, track_len, block_base, damping):
    num_blocks = block_base.shape[0]
    grams = block_grams_kernel(land_jac, pose_jac, segment, knot_frac, track_len, num_blocks, 8)
    group_cols = damping.shape[0]
    num_groups = lax.axis_size("cols")
    band = place_band(skew_blocks(grams), block_base, group_cols, num_groups)
    band_whole = butterfly_sum(scatter_sum(band, "cols"), "rows")
    group_knots = group_cols // KDOF
    yt = band_whole.reshape(group_knots, WIN_KNOTS * KDOF, KDOF).transpose(1, 0, 2)
    yt = yt.reshape(WIN_KNOTS * KDOF, group_cols)
    return band_cholesky(yt, damping, group_cols)


def solution(mesh):
    return jax.shard_map(
        local,
        mesh=mesh,
        in_specs=(
            P(None, None, ("rows", "cols")),
            P(None, None, ("rows", "cols")),
            P(None, ("rows", "cols")),
            P(None, ("rows", "cols")),
            P(("rows", "cols")),
            P(("rows", "cols")),
            P("cols"),
        ),
        out_specs=P("cols", None),
        check_vma=False,
    )
```
